256 devices in a mesh: view: 16 (over z, y_hi), row: 16 (over x, y_lo, core).
Axes of the slice: x: 4, y: 4 (y_hi: 2, y_lo: 2; y = y_hi * 2 + y_lo), z: 8, core: 2. Of those that a mesh axis runs over, the one named last changes fastest.
Arguments:
- latent: bfloat16 [1, 16, 32, 72, 1280], P(None, 'view', 'row'), may hold values from -30 to 30
- gn_gain: float32 [1280], replicated, may hold values from 0.25 to 1.75
- gn_bias: float32 [1280], replicated, may hold values from -3 to 3
- cam_idx: int32 [1, 16], P(None, 'view'), may hold values from 0 to 63
- noise_idx: int32 [1], replicated, may hold values from 0 to 999
- cam_table: bfloat16 [64, 2560], replicated, may hold values from -2 to 2
- noise_table: bfloat16 [1000, 2560], replicated, may hold values from -2 to 2
- conv_w: bfloat16 [3, 3, 1280, 1280], P(None, None, None, 'row'), may hold values from -0.0546875 to 0.0546875
- conv_bias: float32 [1280], replicated, may hold values from -3 to 3
- ln_gain: float32 [1280], replicated, may hold values from 0.25 to 1.75
- attn_in: bfloat16 [3, 1280, 1280], P(None, None, 'view'), may hold values from -0.15625 to 0.15625
- attn_out: bfloat16 [1280, 1280], P('view'), may hold values from -0.15625 to 0.15625
- head_scale: float32 [20], replicated, may hold values from 0.4 to 135
Outputs:
- block_out: bfloat16 [1, 16, 32, 72, 1280], P(None, 'view', 'row')
The draws below stay inside these ranges and needn't reach their ends.
All inputs are finite; a program needn't handle non-finite values.
Results may differ from the reference program's by a relative error of at most 0.02.
Values may be sent and summed in bfloat16 or wider, within the bound.
No kernel may reach another device: no remote copies, remote signals or barrier semaphores. Data moves between devices by JAX's collectives and lax.ppermute only.
A program may use at most 192 MiB of HBM per device.

```python
import math
import jax
import jax.numpy as jnp
from jax import lax

C = 1280
HEADS = 20
HD = 64
GROUPS = 32
WIDTH = 72
NCAM = 64
NLEVEL = 1000
SAMPLES = 1
CO = 1280
VIEWS = 16
HEIGHT = 32


def draw_latent(key, part):
    normal_part = jnp.clip(jax.random.normal(key, (SAMPLES, VIEWS, HEIGHT, WIDTH, C), jnp.float32), -3.5, 3.5)
    row_ramp = 1.0 + 2.0 * jnp.arange(HEIGHT, dtype=jnp.float32) / max(HEIGHT - 1, 1)
    row_ramp = row_ramp[None, None, :, None, None]
    offset = jax.random.uniform(jax.random.fold_in(key, 11), (C,), jnp.float32, 0.4, 1.0)
    return (normal_part * row_ramp + offset * row_ramp).astype(jnp.bfloat16)


def draw_head_scale(key, part):
    ladder = jnp.exp(jnp.linspace(math.log(0.5), math.log(2.0), HEADS))
    order_perm = jax.random.permutation(jax.random.fold_in(key, 3), HEADS)
    jitter = jax.random.uniform(jax.random.fold_in(key, 5), (HEADS,), jnp.float32, 0.9, 1.1)
    return ladder[order_perm] * jitter


def touch_ends(array, own_key, smallest, largest):
    longest = array.shape.index(max(array.shape))
    spots = []
    for shift in (0, 1):
        where = [jax.random.randint(jax.random.fold_in(own_key, axis), (), 0, length) for axis, length in enumerate(array.shape)]
        where[longest] = (where[longest] + shift) % array.shape[longest]
        spots.append(tuple(where))
    return array.at[spots[0]].set(smallest).at[spots[1]].set(largest)


def shard_levels(rng, dims, split, low, largest):
    gain, own = 1.0, jax.random.fold_in(rng, 6)
    for dim, parts in split:
        heights = jnp.exp(jax.random.uniform(jax.random.fold_in(own, dim), (parts,), jnp.float32, low / len(split), largest / len(split)))
        gain = gain * jnp.repeat(heights, dims[dim] // parts).reshape([-1 if axis == dim else 1 for axis in range(len(dims))])
    return gain


def gaussian(key, dims, deviation, reach, split=(), kind=jnp.bfloat16):
    values = jax.random.normal(key, dims, jnp.float32) * deviation
    if len(split) > 0:
        values = shard_levels(key, dims, split, -0.22, 0.18) * values
    return jnp.clip(values, min=-reach, max=reach).astype(kind)


def setup_inputs(seed: int = 0) -> dict:
    seeds = jax.random.split(jax.random.key(seed), 14)
    return {
        "latent": draw_latent(jax.random.fold_in(seeds[13], 71), 0),
        "gn_gain": jnp.clip(1.0 + 0.15 * jax.random.normal(seeds[1], (C,), jnp.float32), 0.25, 1.75),
        "gn_bias": gaussian(seeds[2], (C,), 0.5, 3.0, (), jnp.float32),
        "cam_idx": touch_ends(jax.random.randint(seeds[3], (SAMPLES, VIEWS), 0, NCAM), jax.random.fold_in(seeds[3], 1), 0, NCAM - 1).astype(jnp.int32),
        "noise_idx": jax.random.randint(seeds[4], (SAMPLES,), 0, NLEVEL).astype(jnp.int32),
        "cam_table": gaussian(seeds[5], (NCAM, 2 * C), 0.4, 2.0),
        "noise_table": gaussian(seeds[6], (NLEVEL, 2 * C), 0.4, 2.0),
        "conv_w": gaussian(seeds[7], (3, 3, C, CO), (9 * C) ** -0.5, 0.0546875, ((3, 16),)),
        "conv_bias": gaussian(seeds[8], (CO,), 0.5, 3.0, (), jnp.float32),
        "ln_gain": jnp.clip(1.0 + 0.15 * jax.random.normal(seeds[9], (CO,), jnp.float32), 0.25, 1.75),
        "attn_in": gaussian(seeds[10], (3, CO, CO), CO ** -0.5, 0.15625, ((2, 16),)),
        "attn_out": gaussian(seeds[11], (CO, CO), CO ** -0.5, 0.15625, ((0, 16),)),
        "head_scale": draw_head_scale(jax.random.fold_in(seeds[13], 71), 0),
    }


epsilon = 1e-05

def reference(latent, gn_gain, gn_bias, cam_idx, noise_idx, cam_table, noise_table, conv_w, conv_bias, ln_gain, attn_in, attn_out, head_scale):
    x_float = latent.astype(jnp.float32)
    grouped = x_float.reshape(SAMPLES, VIEWS, HEIGHT, WIDTH, GROUPS, C // GROUPS)
    average = lax.optimization_barrier(jnp.mean(grouped, axis=(2, 3, 5), keepdims=True))
    centred = grouped - average
    variance = lax.optimization_barrier(jnp.mean(centred * centred, axis=(2, 3, 5), keepdims=True))
    normed = (centred * lax.rsqrt(variance + epsilon)).reshape(x_float.shape)
    film_rows = cam_table[cam_idx].astype(jnp.float32) + noise_table[noise_idx].astype(jnp.float32)[:, None, :]
    film_scale = film_rows[:, :, None, None, :C]
    film_shift = film_rows[:, :, None, None, C:]
    hidden = (normed * gn_gain + gn_bias) * (1.0 + film_scale) + film_shift
    activated = jax.nn.silu(hidden).astype(jnp.bfloat16)
    padded = jnp.pad(activated, ((0, 0), (0, 0), (1, 1), (1, 1), (0, 0)))
    conv_out = jnp.zeros((SAMPLES * VIEWS * HEIGHT * WIDTH, CO), jnp.float32)
    for tap_row in range(3):
        for tap_col in range(3):
            tap_rows = padded[:, :, tap_row:tap_row + HEIGHT, tap_col:tap_col + WIDTH, :].reshape(-1, C)
            conv_out = conv_out + jnp.dot(tap_rows, conv_w[tap_row, tap_col], preferred_element_type=jnp.float32)
    conv_out = conv_out.reshape(SAMPLES, VIEWS, HEIGHT, WIDTH, CO)
    resid_out = (x_float + conv_out + conv_bias).astype(jnp.bfloat16)
    resid_float = resid_out.astype(jnp.float32)
    middle = lax.optimization_barrier(jnp.mean(resid_float, axis=-1, keepdims=True))
    spread = lax.optimization_barrier(jnp.mean((resid_float - middle) ** 2, axis=-1, keepdims=True))
    normed_y = ((resid_float - middle) * lax.rsqrt(spread + epsilon) * ln_gain).astype(jnp.bfloat16)
    flat_y = normed_y.reshape(-1, CO)
    head_shape = (SAMPLES, VIEWS, HEIGHT * WIDTH, HEADS, HD)
    query = jnp.dot(flat_y, attn_in[0], preferred_element_type=jnp.float32).astype(jnp.bfloat16).reshape(head_shape)
    key_heads = jnp.dot(flat_y, attn_in[1], preferred_element_type=jnp.float32).astype(jnp.bfloat16).reshape(head_shape)
    value = jnp.dot(flat_y, attn_in[2], preferred_element_type=jnp.float32).astype(jnp.bfloat16).reshape(head_shape)
    scores = jnp.einsum('svphd,suphd->sphvu', query.astype(jnp.float32), key_heads.astype(jnp.float32))
    scores = scores * (head_scale / math.sqrt(HD))[None, None, :, None, None]
    peak_score = lax.optimization_barrier(jnp.max(scores, axis=-1, keepdims=True))
    exp_scores = jnp.exp(scores - peak_score)
    soft_weights = (exp_scores / lax.optimization_barrier(jnp.sum(exp_scores, axis=-1, keepdims=True))).astype(jnp.bfloat16)
    mixed = jnp.einsum('sphvu,suphd->svphd', soft_weights.astype(jnp.float32), value.astype(jnp.float32)).astype(jnp.bfloat16)
    projected = jnp.dot(mixed.reshape(-1, CO), attn_out, preferred_element_type=jnp.float32)
    return (resid_float + projected.reshape(resid_float.shape)).astype(jnp.bfloat16)
```

```python
import math

import jax
import jax.numpy as jnp
from jax import lax
from jax.sharding import PartitionSpec as P

GROUPS = 32


epsilon = 1e-05


def attend(query, key_block, value, head_scale):
    view_count = query.shape[0]
    item_count = query.shape[2]
    channels = query.shape[3]
    head_count = head_scale.shape[0]
    head_size = channels // head_count
    query_heads = query.reshape(view_count, item_count, head_count, head_size)
    key_heads = key_block.reshape(view_count, item_count, head_count, head_size)
    value_heads = value.reshape(view_count, item_count, head_count, head_size)
    scores = jnp.einsum(
        "vihd,uihd->ihvu", query_heads, key_heads, preferred_element_type=jnp.float32
    )
    scores = scores * (head_scale / math.sqrt(head_size))[None, :, None, None]
    peak_score = jnp.max(scores, axis=-1, keepdims=True)
    exp_scores = jnp.exp(scores - peak_score)
    soft_weights = (exp_scores / jnp.sum(exp_scores, axis=-1, keepdims=True)).astype(jnp.bfloat16)
    mixed = jnp.einsum(
        "ihvu,uihd->vihd", soft_weights, value_heads, preferred_element_type=jnp.float32
    )
    return mixed.astype(jnp.bfloat16).reshape(view_count, 1, item_count, channels)


def send_back(mixed):
    return lax.all_to_all(mixed, "view", split_axis=0, concat_axis=1, tiled=True)


def local(
    latent,
    gn_gain,
    gn_bias,
    cam_idx,
    noise_idx,
    cam_table,
    noise_table,
    conv_w,
    conv_bias,
    ln_gain,
    attn_in,
    attn_out,
    head_scale,
):
    samples, local_views, local_rows, local_cols, channels = latent.shape
    width_out = ln_gain.shape[0]
    out_part = conv_w.shape[-1]
    row_devices = lax.axis_size("row")
    whole = lax.all_gather(latent, "row", axis=2, tiled=True)
    whole, attn_in, attn_out = lax.optimization_barrier((whole, attn_in, attn_out))
    weights_in = lax.all_gather(attn_in, "view", axis=0, tiled=False)
    weights_out = lax.all_gather(attn_out, "view", axis=0, tiled=True)

    all_rows = whole.shape[2]
    x_float = whole.astype(jnp.float32)
    grouped = x_float.reshape(
        samples, local_views, all_rows, local_cols, GROUPS, channels // GROUPS
    )
    average = jnp.mean(grouped, axis=(2, 3, 5), keepdims=True)
    centred = grouped - average
    variance = jnp.mean(centred * centred, axis=(2, 3, 5), keepdims=True)
    normed = (centred * lax.rsqrt(variance + epsilon)).reshape(x_float.shape)
    cam_hot = (cam_idx[:, :, None] == jnp.arange(cam_table.shape[0], dtype=jnp.int32)).astype(
        jnp.bfloat16
    )
    cam_film = jnp.einsum("svn,nc->svc", cam_hot, cam_table, preferred_element_type=jnp.float32)
    noise_hot = (noise_idx[:, None] == jnp.arange(noise_table.shape[0], dtype=jnp.int32)).astype(
        jnp.bfloat16
    )
    noise_film = jnp.dot(noise_hot, noise_table, preferred_element_type=jnp.float32)
    film_rows = cam_film + noise_film[:, None, :]
    film_scale = film_rows[:, :, None, None, :channels]
    film_shift = film_rows[:, :, None, None, channels:]
    hidden = (normed * gn_gain + gn_bias) * (1.0 + film_scale) + film_shift
    activated = jax.nn.silu(hidden).astype(jnp.bfloat16)
    conv_out = lax.conv_general_dilated(
        activated.reshape(samples * local_views, all_rows, local_cols, channels),
        conv_w,
        window_strides=(1, 1),
        padding=((1, 1), (1, 1)),
        dimension_numbers=("NHWC", "HWIO", "NHWC"),
        preferred_element_type=jnp.float32,
    ).reshape(samples, local_views, all_rows, local_cols, out_part)
    me = lax.axis_index("row")
    bias_part = lax.dynamic_slice_in_dim(conv_bias, me * out_part, out_part)
    latent_part = lax.dynamic_slice_in_dim(whole, me * out_part, out_part, axis=4)
    resid_part = (latent_part.astype(jnp.float32) + conv_out + bias_part).astype(jnp.bfloat16)
    resid_out = lax.all_to_all(resid_part, "row", split_axis=2, concat_axis=4, tiled=True)
    resid_float = resid_out.astype(jnp.float32)
    middle = jnp.mean(resid_float, axis=-1, keepdims=True)
    spread_y = jnp.mean((resid_float - middle) ** 2, axis=-1, keepdims=True)
    normed_y = ((resid_float - middle) * lax.rsqrt(spread_y + epsilon) * ln_gain).astype(
        jnp.bfloat16
    )
    view_devices = lax.axis_size("view")
    per_device = samples * local_rows * local_cols // view_devices
    pixel_major = jnp.moveaxis(normed_y, 1, 0).reshape(
        local_views, view_devices, per_device, width_out
    )

    def project(pixel_block, matrix_index):
        block_shape = pixel_block.shape
        flat_block = pixel_block.reshape(-1, width_out)
        return (
            jnp.einsum(
                "pc,jcd->pjd",
                flat_block,
                weights_in[:, matrix_index],
                preferred_element_type=jnp.float32,
            )
            .astype(jnp.bfloat16)
            .reshape(block_shape)
        )

    triple_in = (project(pixel_major, 0), project(pixel_major, 1), project(pixel_major, 2))
    mixed = send_back(
        attend(
            lax.all_to_all(triple_in[0], "view", split_axis=1, concat_axis=0, tiled=True),
            lax.all_to_all(triple_in[1], "view", split_axis=1, concat_axis=0, tiled=True),
            lax.all_to_all(triple_in[2], "view", split_axis=1, concat_axis=0, tiled=True),
            head_scale,
        )
    )
    mixed = jnp.moveaxis(
        mixed.reshape(local_views, samples, local_rows, local_cols, width_out), 0, 1
    )
    flat_mixed = mixed.reshape(-1, width_out)
    projected = jnp.dot(flat_mixed, weights_out, preferred_element_type=jnp.float32)
    return (resid_float + projected.reshape(resid_float.shape)).astype(jnp.bfloat16)


def solution(mesh):
    placed = (
        P(None, "view", "row", None, None),
        P(),
        P(),
        P(None, "view"),
        P(),
        P(),
        P(),
        P(None, None, None, "row"),
        P(),
        P(),
        P(None, None, "view"),
        P("view", None),
        P(),
    )
    return jax.shard_map(
        local,
        mesh=mesh,
        in_specs=placed,
        out_specs=P(None, "view", "row", None, None),
        check_vma=False,
    )
```

```python
import math

import jax
import jax.numpy as jnp
from jax import lax
from jax.sharding import PartitionSpec as P

GROUPS = 32


epsilon = 1e-05


def attend(query, key_block, value, head_scale):
    view_count = query.shape[0]
    item_count = query.shape[2]
    channels = query.shape[3]
    head_count = head_scale.shape[0]
    head_size = channels // head_count
    query_heads = query.reshape(view_count, item_count, head_count, head_size)
    key_heads = key_block.reshape(view_count, item_count, head_count, head_size)
    value_heads = value.reshape(view_count, item_count, head_count, head_size)
    scores = jnp.einsum(
        "vihd,uihd->ihvu", query_heads, key_heads, preferred_element_type=jnp.float32
    )
    scores = scores * (head_scale / math.sqrt(head_size))[None, :, None, None]
    peak_score = jnp.max(scores, axis=-1, keepdims=True)
    exp_scores = jnp.exp(scores - peak_score)
    soft_weights = (exp_scores / jnp.sum(exp_scores, axis=-1, keepdims=True)).astype(jnp.bfloat16)
    mixed = jnp.einsum(
        "ihvu,uihd->vihd", soft_weights, value_heads, preferred_element_type=jnp.float32
    )
    return mixed.astype(jnp.bfloat16).reshape(view_count, 1, item_count, channels)


def send_back(mixed):
    return lax.all_to_all(mixed, "view", split_axis=0, concat_axis=1, tiled=True)


def local(
    latent,
    gn_gain,
    gn_bias,
    cam_idx,
    noise_idx,
    cam_table,
    noise_table,
    conv_w,
    conv_bias,
    ln_gain,
    attn_in,
    attn_out,
    head_scale,
):
    samples, local_views, local_rows, local_cols, channels = latent.shape
    width_out = ln_gain.shape[0]
    out_part = conv_w.shape[-1]
    whole = lax.all_gather(latent, ROW, axis=2, tiled=True)
    whole, attn_in, attn_out = lax.optimization_barrier((whole, attn_in, attn_out))
    core = lax.axis_index("core")
    half_in = attn_in.shape[1] // 2
    half_out = attn_out.shape[1] // 2
    in_half = lax.dynamic_slice_in_dim(attn_in, core * half_in, half_in, axis=1)
    in_half = lax.all_gather(in_half, "view", axis=0, tiled=False)
    out_half = lax.dynamic_slice_in_dim(attn_out, core * half_out, half_out, axis=1)

    all_rows = whole.shape[2]
    x_float = whole.astype(jnp.float32)
    grouped = x_float.reshape(
        samples, local_views, all_rows, local_cols, GROUPS, channels // GROUPS
    )
    average = jnp.mean(grouped, axis=(2, 3, 5), keepdims=True)
    centred = grouped - average
    variance = jnp.mean(centred * centred, axis=(2, 3, 5), keepdims=True)
    normed = (centred * lax.rsqrt(variance + epsilon)).reshape(x_float.shape)
    cam_hot = (cam_idx[:, :, None] == jnp.arange(cam_table.shape[0], dtype=jnp.int32)).astype(
        jnp.bfloat16
    )
    cam_film = jnp.einsum("svn,nc->svc", cam_hot, cam_table, preferred_element_type=jnp.float32)
    noise_hot = (noise_idx[:, None] == jnp.arange(noise_table.shape[0], dtype=jnp.int32)).astype(
        jnp.bfloat16
    )
    noise_film = jnp.dot(noise_hot, noise_table, preferred_element_type=jnp.float32)
    film_rows = cam_film + noise_film[:, None, :]
    film_scale = film_rows[:, :, None, None, :channels]
    film_shift = film_rows[:, :, None, None, channels:]
    hidden = (normed * gn_gain + gn_bias) * (1.0 + film_scale) + film_shift
    activated = jax.nn.silu(hidden).astype(jnp.bfloat16)
    conv_out = lax.conv_general_dilated(
        activated.reshape(samples * local_views, all_rows, local_cols, channels),
        conv_w,
        window_strides=(1, 1),
        padding=((1, 1), (1, 1)),
        dimension_numbers=("NHWC", "HWIO", "NHWC"),
        preferred_element_type=jnp.float32,
    ).reshape(samples, local_views, all_rows, local_cols, out_part)
    me = lax.axis_index("chip") * lax.axis_size("core") + core
    bias_part = lax.dynamic_slice_in_dim(conv_bias, me * out_part, out_part)
    latent_part = lax.dynamic_slice_in_dim(whole, me * out_part, out_part, axis=4)
    resid_part = (latent_part.astype(jnp.float32) + conv_out + bias_part).astype(jnp.bfloat16)
    in_half, resid_part = lax.optimization_barrier((in_half, resid_part))
    weights_in = lax.all_gather(in_half, "core", axis=0, tiled=False)
    resid_out = lax.all_to_all(resid_part, ROW, split_axis=2, concat_axis=4, tiled=True)
    resid_float = resid_out.astype(jnp.float32)
    middle = jnp.mean(resid_float, axis=-1, keepdims=True)
    spread_y = jnp.mean((resid_float - middle) ** 2, axis=-1, keepdims=True)
    normed_y = ((resid_float - middle) * lax.rsqrt(spread_y + epsilon) * ln_gain).astype(
        jnp.bfloat16
    )
    view_devices = lax.axis_size("view")
    per_device = samples * local_rows * local_cols // view_devices
    pixel_major = jnp.moveaxis(normed_y, 1, 0).reshape(
        local_views, view_devices, per_device, width_out
    )

    flat_block = pixel_major.reshape(-1, 2, width_out // 2)
    triple_in = jnp.einsum(
        "pkc,kjmcd->mpjd", flat_block, weights_in, preferred_element_type=jnp.float32
    ).astype(jnp.bfloat16)
    triple_in = triple_in.reshape((3,) + pixel_major.shape)
    out_half, triple_in = lax.optimization_barrier((out_half, triple_in))
    out_half = lax.all_gather(out_half, "view", axis=0, tiled=True)
    triple_in = lax.all_to_all(triple_in, "view", split_axis=2, concat_axis=1, tiled=True)
    mixed = send_back(attend(triple_in[0], triple_in[1], triple_in[2], head_scale))
    out_half, mixed = lax.optimization_barrier((out_half, mixed))
    weights_out = lax.all_gather(out_half, "core", axis=0, tiled=False)
    mixed = jnp.moveaxis(
        mixed.reshape(local_views, samples, local_rows, local_cols, width_out), 0, 1
    )
    flat_mixed = mixed.reshape(-1, width_out)
    projected = jnp.einsum(
        "pc,kcd->pkd", flat_mixed, weights_out, preferred_element_type=jnp.float32
    )
    return (resid_float + projected.reshape(resid_float.shape)).astype(jnp.bfloat16)


ROW = ("chip", "core")


def solution(mesh):
    cores = 2
    split = jax.sharding.Mesh(
        mesh.devices.reshape(mesh.shape["view"], mesh.shape["row"] // cores, cores),
        ("view", "chip", "core"),
    )
    placed = (
        P(None, "view", ROW, None, None),
        P(),
        P(),
        P(None, "view"),
        P(),
        P(),
        P(),
        P(None, None, None, ROW),
        P(),
        P(),
        P(None, None, "view"),
        P("view", None),
        P(),
    )
    return jax.shard_map(
        local,
        mesh=split,
        in_specs=placed,
        out_specs=P(None, "view", ROW, None, None),
        check_vma=False,
    )
```

```python
import math

import jax
import jax.numpy as jnp
from jax import lax
from jax.sharding import PartitionSpec as P

GROUPS = 32


epsilon = 1e-05


def attend(query, key_block, value, head_scale):
    view_count = query.shape[0]
    item_count = query.shape[2]
    channels = query.shape[3]
    head_count = head_scale.shape[0]
    head_size = channels // head_count
    query_heads = query.reshape(view_count, item_count, head_count, head_size)
    key_heads = key_block.reshape(view_count, item_count, head_count, head_size)
    value_heads = value.reshape(view_count, item_count, head_count, head_size)
    scores = jnp.einsum(
        "vihd,uihd->ihvu", query_heads, key_heads, preferred_element_type=jnp.float32
    )
    scores = scores * (head_scale / math.sqrt(head_size))[None, :, None, None]
    peak_score = jnp.max(scores, axis=-1, keepdims=True)
    exp_scores = jnp.exp(scores - peak_score)
    soft_weights = (exp_scores / jnp.sum(exp_scores, axis=-1, keepdims=True)).astype(jnp.bfloat16)
    mixed = jnp.einsum(
        "ihvu,uihd->vihd", soft_weights, value_heads, preferred_element_type=jnp.float32
    )
    return mixed.astype(jnp.bfloat16).reshape(view_count, 1, item_count, channels)


def send_back(mixed):
    return lax.all_to_all(mixed, VIEW, split_axis=0, concat_axis=1, tiled=True)


def local(
    latent,
    gn_gain,
    gn_bias,
    cam_idx,
    noise_idx,
    cam_table,
    noise_table,
    conv_w,
    conv_bias,
    ln_gain,
    attn_in,
    attn_out,
    head_scale,
):
    samples, local_views, local_rows, local_cols, channels = latent.shape
    width_out = ln_gain.shape[0]
    out_part = conv_w.shape[-1]
    whole = lax.all_gather(latent, ROW, axis=2, tiled=True)
    whole, attn_in, attn_out = lax.optimization_barrier((whole, attn_in, attn_out))
    core = lax.axis_index("core")
    half_in = attn_in.shape[1] // 2
    half_out = attn_out.shape[1] // 2
    in_half = lax.dynamic_slice_in_dim(attn_in, core * half_in, half_in, axis=1)
    in_half = lax.all_gather(in_half, "vz", axis=0, tiled=False)
    in_half = lax.all_gather(in_half, "vy", axis=0, tiled=False)
    out_half = lax.dynamic_slice_in_dim(attn_out, core * half_out, half_out, axis=1)

    all_rows = whole.shape[2]
    x_float = whole.astype(jnp.float32)
    grouped = x_float.reshape(
        samples, local_views, all_rows, local_cols, GROUPS, channels // GROUPS
    )
    average = jnp.mean(grouped, axis=(2, 3, 5), keepdims=True)
    centred = grouped - average
    variance = jnp.mean(centred * centred, axis=(2, 3, 5), keepdims=True)
    normed = (centred * lax.rsqrt(variance + epsilon)).reshape(x_float.shape)
    cam_hot = (cam_idx[:, :, None] == jnp.arange(cam_table.shape[0], dtype=jnp.int32)).astype(
        jnp.bfloat16
    )
    cam_film = jnp.einsum("svn,nc->svc", cam_hot, cam_table, preferred_element_type=jnp.float32)
    noise_hot = (noise_idx[:, None] == jnp.arange(noise_table.shape[0], dtype=jnp.int32)).astype(
        jnp.bfloat16
    )
    noise_film = jnp.dot(noise_hot, noise_table, preferred_element_type=jnp.float32)
    film_rows = cam_film + noise_film[:, None, :]
    film_scale = film_rows[:, :, None, None, :channels]
    film_shift = film_rows[:, :, None, None, channels:]
    hidden = (normed * gn_gain + gn_bias) * (1.0 + film_scale) + film_shift
    activated = jax.nn.silu(hidden).astype(jnp.bfloat16)
    conv_out = lax.conv_general_dilated(
        activated.reshape(samples * local_views, all_rows, local_cols, channels),
        conv_w,
        window_strides=(1, 1),
        padding=((1, 1), (1, 1)),
        dimension_numbers=("NHWC", "HWIO", "NHWC"),
        preferred_element_type=jnp.float32,
    ).reshape(samples, local_views, all_rows, local_cols, out_part)
    me = lax.axis_index("chip") * lax.axis_size("core") + core
    bias_part = lax.dynamic_slice_in_dim(conv_bias, me * out_part, out_part)
    latent_part = lax.dynamic_slice_in_dim(whole, me * out_part, out_part, axis=4)
    resid_part = (latent_part.astype(jnp.float32) + conv_out + bias_part).astype(jnp.bfloat16)
    in_half, resid_part = lax.optimization_barrier((in_half, resid_part))
    swap = [(0, 1), (1, 0)]
    in_other = lax.ppermute(in_half, "core", swap)
    resid_out = lax.all_to_all(resid_part, ROW, split_axis=2, concat_axis=4, tiled=True)
    resid_float = resid_out.astype(jnp.float32)
    middle = jnp.mean(resid_float, axis=-1, keepdims=True)
    spread_y = jnp.mean((resid_float - middle) ** 2, axis=-1, keepdims=True)
    normed_y = ((resid_float - middle) * lax.rsqrt(spread_y + epsilon) * ln_gain).astype(
        jnp.bfloat16
    )
    view_devices = lax.axis_size(VIEW)
    per_device = samples * local_rows * local_cols // view_devices
    pixel_major = jnp.moveaxis(normed_y, 1, 0).reshape(
        local_views, view_devices, per_device, width_out
    )

    flat_block = pixel_major.reshape(-1, width_out)
    block_mine = lax.dynamic_slice_in_dim(flat_block, core * half_in, half_in, axis=1)
    block_other = lax.dynamic_slice_in_dim(flat_block, (1 - core) * half_in, half_in, axis=1)
    triple_in = jnp.einsum(
        "pc,yzmcd->mpzyd", block_mine, in_half, preferred_element_type=jnp.float32
    ) + jnp.einsum(
        "pc,yzmcd->mpzyd", block_other, in_other, preferred_element_type=jnp.float32
    )
    triple_in = triple_in.astype(jnp.bfloat16)
    triple_in = triple_in.reshape((3,) + pixel_major.shape)
    out_half, triple_in = lax.optimization_barrier((out_half, triple_in))
    out_half = lax.all_gather(out_half, "vz", axis=0, tiled=False)
    out_half = lax.all_gather(out_half, "vy", axis=0, tiled=False)
    triple_in = lax.all_to_all(triple_in, VIEW, split_axis=2, concat_axis=1, tiled=True)
    mixed = send_back(attend(triple_in[0], triple_in[1], triple_in[2], head_scale))
    out_half, mixed = lax.optimization_barrier((out_half, mixed))
    out_other = lax.ppermute(out_half, "core", swap)
    mixed = jnp.moveaxis(
        mixed.reshape(local_views, samples, local_rows, local_cols, width_out), 0, 1
    )
    flat_mixed = mixed.reshape(-1, lax.axis_size("vz"), lax.axis_size("vy"), out_half.shape[2])
    cols_mine = jnp.einsum(
        "pzyr,yzrd->pd", flat_mixed, out_half, preferred_element_type=jnp.float32
    )
    cols_other = jnp.einsum(
        "pzyr,yzrd->pd", flat_mixed, out_other, preferred_element_type=jnp.float32
    )
    projected = jnp.where(
        core == 0,
        jnp.concatenate([cols_mine, cols_other], axis=1),
        jnp.concatenate([cols_other, cols_mine], axis=1),
    )
    return (resid_float + projected.reshape(resid_float.shape)).astype(jnp.bfloat16)


ROW = ("chip", "core")
VIEW = ("vz", "vy")


def solution(mesh):
    cores = 2
    split = jax.sharding.Mesh(
        mesh.devices.reshape(
            mesh.shape["view"] // 2, 2, mesh.shape["row"] // cores, cores
        ),
        ("vz", "vy", "chip", "core"),
    )
    placed = (
        P(None, VIEW, ROW, None, None),
        P(),
        P(),
        P(None, VIEW),
        P(),
        P(),
        P(),
        P(None, None, None, ROW),
        P(),
        P(),
        P(None, None, VIEW),
        P(VIEW, None),
        P(),
    )
    return jax.shard_map(
        local,
        mesh=split,
        in_specs=placed,
        out_specs=P(None, VIEW, ROW, None, None),
        check_vma=False,
    )
```

```python
import math

import jax
import jax.numpy as jnp
from jax import lax
from jax.sharding import PartitionSpec as P

GROUPS = 32


epsilon = 1e-05


def attend(query, key_block, value, head_scale):
    view_count = query.shape[0]
    item_count = query.shape[2]
    channels = query.shape[3]
    head_count = head_scale.shape[0]
    head_size = channels // head_count
    query_heads = query.reshape(view_count, item_count, head_count, head_size)
    key_heads = key_block.reshape(view_count, item_count, head_count, head_size)
    value_heads = value.reshape(view_count, item_count, head_count, head_size)
    scores = jnp.einsum(
        "vihd,uihd->ihvu", query_heads, key_heads, preferred_element_type=jnp.float32
    )
    scores = scores * (head_scale / math.sqrt(head_size))[None, :, None, None]
    peak_score = jnp.max(scores, axis=-1, keepdims=True)
    exp_scores = jnp.exp(scores - peak_score)
    soft_weights = (exp_scores / jnp.sum(exp_scores, axis=-1, keepdims=True)).astype(jnp.bfloat16)
    mixed = jnp.einsum(
        "ihvu,uihd->vihd", soft_weights, value_heads, preferred_element_type=jnp.float32
    )
    return mixed.astype(jnp.bfloat16).reshape(view_count, 1, item_count, channels)


def send_back(mixed):
    return lax.all_to_all(mixed, VIEW, split_axis=0, concat_axis=1, tiled=True)


def local(
    latent,
    gn_gain,
    gn_bias,
    cam_idx,
    noise_idx,
    cam_table,
    noise_table,
    conv_w,
    conv_bias,
    ln_gain,
    attn_in,
    attn_out,
    head_scale,
):
    samples, local_views, local_rows, local_cols, channels = latent.shape
    width_out = ln_gain.shape[0]
    out_part = conv_w.shape[-1]
    whole = lax.all_gather(latent, ROW, axis=2, tiled=True)
    whole, attn_in, attn_out = lax.optimization_barrier((whole, attn_in, attn_out))
    core = lax.axis_index("core")
    half_in = attn_in.shape[1] // 2
    half_out = attn_out.shape[1] // 2
    in_half = lax.dynamic_slice_in_dim(attn_in, core * half_in, half_in, axis=1)
    in_half = lax.all_gather(in_half, VIEW, axis=0, tiled=False)
    out_half = lax.dynamic_slice_in_dim(attn_out, core * half_out, half_out, axis=1)

    all_rows = whole.shape[2]
    x_float = whole.astype(jnp.float32)
    grouped = x_float.reshape(
        samples, local_views, all_rows, local_cols, GROUPS, channels // GROUPS
    )
    average = jnp.mean(grouped, axis=(2, 3, 5), keepdims=True)
    centred = grouped - average
    variance = jnp.mean(centred * centred, axis=(2, 3, 5), keepdims=True)
    normed = (centred * lax.rsqrt(variance + epsilon)).reshape(x_float.shape)
    cam_hot = (cam_idx[:, :, None] == jnp.arange(cam_table.shape[0], dtype=jnp.int32)).astype(
        jnp.bfloat16
    )
    cam_film = jnp.einsum("svn,nc->svc", cam_hot, cam_table, preferred_element_type=jnp.float32)
    noise_hot = (noise_idx[:, None] == jnp.arange(noise_table.shape[0], dtype=jnp.int32)).astype(
        jnp.bfloat16
    )
    noise_film = jnp.dot(noise_hot, noise_table, preferred_element_type=jnp.float32)
    film_rows = cam_film + noise_film[:, None, :]
    film_scale = film_rows[:, :, None, None, :channels]
    film_shift = film_rows[:, :, None, None, channels:]
    hidden = (normed * gn_gain + gn_bias) * (1.0 + film_scale) + film_shift
    activated = jax.nn.silu(hidden).astype(jnp.bfloat16)
    conv_out = lax.conv_general_dilated(
        activated.reshape(samples * local_views, all_rows, local_cols, channels),
        conv_w,
        window_strides=(1, 1),
        padding=((1, 1), (1, 1)),
        dimension_numbers=("NHWC", "HWIO", "NHWC"),
        preferred_element_type=jnp.float32,
    ).reshape(samples, local_views, all_rows, local_cols, out_part)
    me = lax.axis_index("chip") * lax.axis_size("core") + core
    bias_part = lax.dynamic_slice_in_dim(conv_bias, me * out_part, out_part)
    latent_part = lax.dynamic_slice_in_dim(whole, me * out_part, out_part, axis=4)
    resid_part = (latent_part.astype(jnp.float32) + conv_out + bias_part).astype(jnp.bfloat16)
    out_half, resid_part = lax.optimization_barrier((out_half, resid_part))
    out_half = lax.all_gather(out_half, VIEW, axis=0, tiled=True)
    resid_out = lax.all_to_all(resid_part, ROW, split_axis=2, concat_axis=4, tiled=True)
    resid_float = resid_out.astype(jnp.float32)
    middle = jnp.mean(resid_float, axis=-1, keepdims=True)
    spread_y = jnp.mean((resid_float - middle) ** 2, axis=-1, keepdims=True)
    normed_y = ((resid_float - middle) * lax.rsqrt(spread_y + epsilon) * ln_gain).astype(
        jnp.bfloat16
    )
    view_devices = lax.axis_size(VIEW)
    per_device = samples * local_rows * local_cols // view_devices
    pixel_major = jnp.moveaxis(normed_y, 1, 0).reshape(
        local_views, view_devices, per_device, width_out
    )
    views = lax.all_to_all(pixel_major, VIEW, split_axis=1, concat_axis=0, tiled=True)
    in_half, views = lax.optimization_barrier((in_half, views))
    swap = [(0, 1), (1, 0)]
    in_other = lax.ppermute(in_half, "core", swap)
    flat_block = views.reshape(-1, width_out)
    block_mine = lax.dynamic_slice_in_dim(flat_block, core * half_in, half_in, axis=1)
    block_other = lax.dynamic_slice_in_dim(flat_block, (1 - core) * half_in, half_in, axis=1)
    triple_in = jnp.einsum(
        "pc,jmcd->mpjd", block_mine, in_half, preferred_element_type=jnp.float32
    ) + jnp.einsum(
        "pc,jmcd->mpjd", block_other, in_other, preferred_element_type=jnp.float32
    )
    triple_in = triple_in.astype(jnp.bfloat16).reshape((3,) + views.shape)
    mixed = send_back(attend(triple_in[0], triple_in[1], triple_in[2], head_scale))
    out_half, mixed = lax.optimization_barrier((out_half, mixed))
    out_other = lax.ppermute(out_half, "core", swap)
    mixed = jnp.moveaxis(
        mixed.reshape(local_views, samples, local_rows, local_cols, width_out), 0, 1
    )
    flat_mixed = mixed.reshape(-1, width_out)
    cols_mine = jnp.dot(flat_mixed, out_half, preferred_element_type=jnp.float32)
    cols_other = jnp.dot(flat_mixed, out_other, preferred_element_type=jnp.float32)
    projected = jnp.where(
        core == 0,
        jnp.concatenate([cols_mine, cols_other], axis=1),
        jnp.concatenate([cols_other, cols_mine], axis=1),
    )
    return (resid_float + projected.reshape(resid_float.shape)).astype(jnp.bfloat16)

ROW = ("chip", "core")
VIEW = ("vz", "vy")


def solution(mesh):
    cores = 2
    split = jax.sharding.Mesh(
        mesh.devices.reshape(
            mesh.shape["view"] // 2, 2, mesh.shape["row"] // cores, cores
        ),
        ("vz", "vy", "chip", "core"),
    )
    placed = (
        P(None, VIEW, ROW, None, None),
        P(),
        P(),
        P(None, VIEW),
        P(),
        P(),
        P(),
        P(None, None, None, ROW),
        P(),
        P(),
        P(None, None, VIEW),
        P(VIEW, None),
        P(),
    )
    return jax.shard_map(
        local,
        mesh=split,
        in_specs=placed,
        out_specs=P(None, VIEW, ROW, None, None),
        check_vma=False,
    )
```

```python
import math

import jax
import jax.numpy as jnp
from jax import lax
from jax.sharding import PartitionSpec as P

GROUPS = 32


epsilon = 1e-05


def attend(query, key_block, value, head_scale):
    view_count = query.shape[0]
    item_count = query.shape[2]
    channels = query.shape[3]
    head_count = head_scale.shape[0]
    head_size = channels // head_count
    query_heads = query.reshape(view_count, item_count, head_count, head_size)
    key_heads = key_block.reshape(view_count, item_count, head_count, head_size)
    value_heads = value.reshape(view_count, item_count, head_count, head_size)
    scores = jnp.einsum(
        "vihd,uihd->ihvu", query_heads, key_heads, preferred_element_type=jnp.float32
    )
    scores = scores * (head_scale / math.sqrt(head_size))[None, :, None, None]
    peak_score = jnp.max(scores, axis=-1, keepdims=True)
    exp_scores = jnp.exp(scores - peak_score)
    soft_weights = (exp_scores / jnp.sum(exp_scores, axis=-1, keepdims=True)).astype(jnp.bfloat16)
    mixed = jnp.einsum(
        "ihvu,uihd->vihd", soft_weights, value_heads, preferred_element_type=jnp.float32
    )
    return mixed.astype(jnp.bfloat16).reshape(view_count, 1, item_count, channels)


def send_back(mixed):
    return lax.all_to_all(mixed, VIEW, split_axis=0, concat_axis=1, tiled=True)


def local(
    latent,
    gn_gain,
    gn_bias,
    cam_idx,
    noise_idx,
    cam_table,
    noise_table,
    conv_w,
    conv_bias,
    ln_gain,
    attn_in,
    attn_out,
    head_scale,
):
    samples, local_views, local_rows, local_cols, channels = latent.shape
    width_out = ln_gain.shape[0]
    out_part = conv_w.shape[-1]
    whole = lax.all_gather(latent, ROW, axis=2, tiled=True)
    whole, attn_in, attn_out = lax.optimization_barrier((whole, attn_in, attn_out))
    core = lax.axis_index("core")
    half_in = attn_in.shape[1] // 2
    half_out = attn_out.shape[1] // 2
    in_half = lax.dynamic_slice_in_dim(attn_in, core * half_in, half_in, axis=1)
    in_half = lax.all_gather(in_half, VIEW, axis=0, tiled=False)
    out_half = lax.dynamic_slice_in_dim(attn_out, core * half_out, half_out, axis=1)
    view_devices = lax.axis_size(VIEW)
    out_half = jnp.broadcast_to(out_half[None], (view_devices,) + out_half.shape)
    out_half = lax.all_to_all(out_half, VIEW, split_axis=0, concat_axis=0, tiled=True)
    out_half = out_half.reshape(-1, half_out)

    all_rows = whole.shape[2]
    x_float = whole.astype(jnp.float32)
    grouped = x_float.reshape(
        samples, local_views, all_rows, local_cols, GROUPS, channels // GROUPS
    )
    average = jnp.mean(grouped, axis=(2, 3, 5), keepdims=True)
    centred = grouped - average
    variance = jnp.mean(centred * centred, axis=(2, 3, 5), keepdims=True)
    normed = (centred * lax.rsqrt(variance + epsilon)).reshape(x_float.shape)
    cam_hot = (cam_idx[:, :, None] == jnp.arange(cam_table.shape[0], dtype=jnp.int32)).astype(
        jnp.bfloat16
    )
    cam_film = jnp.einsum("svn,nc->svc", cam_hot, cam_table, preferred_element_type=jnp.float32)
    noise_hot = (noise_idx[:, None] == jnp.arange(noise_table.shape[0], dtype=jnp.int32)).astype(
        jnp.bfloat16
    )
    noise_film = jnp.dot(noise_hot, noise_table, preferred_element_type=jnp.float32)
    film_rows = cam_film + noise_film[:, None, :]
    film_scale = film_rows[:, :, None, None, :channels]
    film_shift = film_rows[:, :, None, None, channels:]
    hidden = (normed * gn_gain + gn_bias) * (1.0 + film_scale) + film_shift
    activated = jax.nn.silu(hidden).astype(jnp.bfloat16)
    conv_out = lax.conv_general_dilated(
        activated.reshape(samples * local_views, all_rows, local_cols, channels),
        conv_w,
        window_strides=(1, 1),
        padding=((1, 1), (1, 1)),
        dimension_numbers=("NHWC", "HWIO", "NHWC"),
        preferred_element_type=jnp.float32,
    ).reshape(samples, local_views, all_rows, local_cols, out_part)
    me = lax.axis_index("chip") * lax.axis_size("core") + core
    bias_part = lax.dynamic_slice_in_dim(conv_bias, me * out_part, out_part)
    latent_part = lax.dynamic_slice_in_dim(whole, me * out_part, out_part, axis=4)
    resid_part = (latent_part.astype(jnp.float32) + conv_out + bias_part).astype(jnp.bfloat16)
    resid_out = lax.all_to_all(resid_part, ROW, split_axis=2, concat_axis=4, tiled=True)
    resid_float = resid_out.astype(jnp.float32)
    middle = jnp.mean(resid_float, axis=-1, keepdims=True)
    spread_y = jnp.mean((resid_float - middle) ** 2, axis=-1, keepdims=True)
    normed_y = ((resid_float - middle) * lax.rsqrt(spread_y + epsilon) * ln_gain).astype(
        jnp.bfloat16
    )
    view_devices = lax.axis_size(VIEW)
    per_device = samples * local_rows * local_cols // view_devices
    pixel_major = jnp.moveaxis(normed_y, 1, 0).reshape(
        local_views, view_devices, per_device, width_out
    )
    views = lax.all_to_all(pixel_major, VIEW, split_axis=1, concat_axis=0, tiled=True)
    in_half, views = lax.optimization_barrier((in_half, views))
    swap = [(0, 1), (1, 0)]
    in_other = lax.ppermute(in_half, "core", swap)
    flat_block = views.reshape(-1, width_out)
    block_mine = lax.dynamic_slice_in_dim(flat_block, core * half_in, half_in, axis=1)
    block_other = lax.dynamic_slice_in_dim(flat_block, (1 - core) * half_in, half_in, axis=1)
    triple_in = jnp.einsum(
        "pc,jmcd->mpjd", block_mine, in_half, preferred_element_type=jnp.float32
    ) + jnp.einsum(
        "pc,jmcd->mpjd", block_other, in_other, preferred_element_type=jnp.float32
    )
    triple_in = triple_in.astype(jnp.bfloat16).reshape((3,) + views.shape)
    mixed = send_back(attend(triple_in[0], triple_in[1], triple_in[2], head_scale))
    out_half, mixed = lax.optimization_barrier((out_half, mixed))
    out_other = lax.ppermute(out_half, "core", swap)
    mixed = jnp.moveaxis(
        mixed.reshape(local_views, samples, local_rows, local_cols, width_out), 0, 1
    )
    flat_mixed = mixed.reshape(-1, width_out)
    cols_mine = jnp.dot(flat_mixed, out_half, preferred_element_type=jnp.float32)
    cols_other = jnp.dot(flat_mixed, out_other, preferred_element_type=jnp.float32)
    projected = jnp.where(
        core == 0,
        jnp.concatenate([cols_mine, cols_other], axis=1),
        jnp.concatenate([cols_other, cols_mine], axis=1),
    )
    return (resid_float + projected.reshape(resid_float.shape)).astype(jnp.bfloat16)

ROW = ("chip", "core")
VIEW = ("vz", "vy")


def solution(mesh):
    cores = 2
    split = jax.sharding.Mesh(
        mesh.devices.reshape(
            mesh.shape["view"] // 2, 2, mesh.shape["row"] // cores, cores
        ),
        ("vz", "vy", "chip", "core"),
    )
    placed = (
        P(None, VIEW, ROW, None, None),
        P(),
        P(),
        P(None, VIEW),
        P(),
        P(),
        P(),
        P(None, None, None, ROW),
        P(),
        P(),
        P(None, None, VIEW),
        P(VIEW, None),
        P(),
    )
    return jax.shard_map(
        local,
        mesh=split,
        in_specs=placed,
        out_specs=P(None, VIEW, ROW, None, None),
        check_vma=False,
    )
```

```python
import math

import jax
import jax.numpy as jnp
from jax import lax
from jax.sharding import PartitionSpec as P

GROUPS = 32


epsilon = 1e-05


def attend(query, key_block, value, head_scale):
    view_count = query.shape[0]
    item_count = query.shape[2]
    channels = query.shape[3]
    head_count = head_scale.shape[0]
    head_size = channels // head_count
    query_heads = query.reshape(view_count, item_count, head_count, head_size)
    key_heads = key_block.reshape(view_count, item_count, head_count, head_size)
    value_heads = value.reshape(view_count, item_count, head_count, head_size)
    scores = jnp.einsum(
        "vihd,uihd->ihvu", query_heads, key_heads, preferred_element_type=jnp.float32
    )
    scores = scores * (head_scale / math.sqrt(head_size))[None, :, None, None]
    peak_score = jnp.max(scores, axis=-1, keepdims=True)
    exp_scores = jnp.exp(scores - peak_score)
    soft_weights = (exp_scores / jnp.sum(exp_scores, axis=-1, keepdims=True)).astype(jnp.bfloat16)
    mixed = jnp.einsum(
        "ihvu,uihd->vihd", soft_weights, value_heads, preferred_element_type=jnp.float32
    )
    return mixed.astype(jnp.bfloat16).reshape(view_count, 1, item_count, channels)


def send_back(mixed):
    return lax.all_to_all(mixed, VIEW, split_axis=0, concat_axis=1, tiled=True)


def local(
    latent,
    gn_gain,
    gn_bias,
    cam_idx,
    noise_idx,
    cam_table,
    noise_table,
    conv_w,
    conv_bias,
    ln_gain,
    attn_in,
    attn_out,
    head_scale,
):
    samples, local_views, local_rows, local_cols, channels = latent.shape
    width_out = ln_gain.shape[0]
    out_part = conv_w.shape[-1]
    whole = lax.all_gather(latent, ROW, axis=2, tiled=True)
    whole, attn_in = lax.optimization_barrier((whole, attn_in))
    core = lax.axis_index("core")
    half_in = attn_in.shape[1] // 2
    half_out = attn_out.shape[1] // 2
    in_half = lax.dynamic_slice_in_dim(attn_in, core * half_in, half_in, axis=1)
    in_half = lax.all_gather(in_half, VIEW, axis=0, tiled=False)
    out_half = lax.dynamic_slice_in_dim(attn_out, core * half_out, half_out, axis=1)
    view_devices = lax.axis_size(VIEW)
    out_half = jnp.broadcast_to(out_half[None], (view_devices,) + out_half.shape)
    out_half = lax.all_to_all(out_half, VIEW, split_axis=0, concat_axis=0, tiled=True)
    out_half = out_half.reshape(-1, half_out)

    all_rows = whole.shape[2]
    x_float = whole.astype(jnp.float32)
    grouped = x_float.reshape(
        samples, local_views, all_rows, local_cols, GROUPS, channels // GROUPS
    )
    average = jnp.mean(grouped, axis=(2, 3, 5), keepdims=True)
    centred = grouped - average
    variance = jnp.mean(centred * centred, axis=(2, 3, 5), keepdims=True)
    normed = (centred * lax.rsqrt(variance + epsilon)).reshape(x_float.shape)
    cam_hot = (cam_idx[:, :, None] == jnp.arange(cam_table.shape[0], dtype=jnp.int32)).astype(
        jnp.bfloat16
    )
    cam_film = jnp.einsum("svn,nc->svc", cam_hot, cam_table, preferred_element_type=jnp.float32)
    noise_hot = (noise_idx[:, None] == jnp.arange(noise_table.shape[0], dtype=jnp.int32)).astype(
        jnp.bfloat16
    )
    noise_film = jnp.dot(noise_hot, noise_table, preferred_element_type=jnp.float32)
    film_rows = cam_film + noise_film[:, None, :]
    film_scale = film_rows[:, :, None, None, :channels]
    film_shift = film_rows[:, :, None, None, channels:]
    hidden = (normed * gn_gain + gn_bias) * (1.0 + film_scale) + film_shift
    activated = jax.nn.silu(hidden).astype(jnp.bfloat16)
    out_half, activated = lax.optimization_barrier((out_half, activated))
    conv_out = lax.conv_general_dilated(
        activated.reshape(samples * local_views, all_rows, local_cols, channels),
        conv_w,
        window_strides=(1, 1),
        padding=((1, 1), (1, 1)),
        dimension_numbers=("NHWC", "HWIO", "NHWC"),
        preferred_element_type=jnp.float32,
    ).reshape(samples, local_views, all_rows, local_cols, out_part)
    me = lax.axis_index("chip") * lax.axis_size("core") + core
    bias_part = lax.dynamic_slice_in_dim(conv_bias, me * out_part, out_part)
    latent_part = lax.dynamic_slice_in_dim(whole, me * out_part, out_part, axis=4)
    resid_part = (latent_part.astype(jnp.float32) + conv_out + bias_part).astype(jnp.bfloat16)
    resid_out = lax.all_to_all(resid_part, ROW, split_axis=2, concat_axis=4, tiled=True)
    resid_float = resid_out.astype(jnp.float32)
    middle = jnp.mean(resid_float, axis=-1, keepdims=True)
    spread_y = jnp.mean((resid_float - middle) ** 2, axis=-1, keepdims=True)
    normed_y = ((resid_float - middle) * lax.rsqrt(spread_y + epsilon) * ln_gain).astype(
        jnp.bfloat16
    )
    view_devices = lax.axis_size(VIEW)
    per_device = samples * local_rows * local_cols // view_devices
    pixel_major = jnp.moveaxis(normed_y, 1, 0).reshape(
        local_views, view_devices, per_device, width_out
    )
    views = lax.all_to_all(pixel_major, VIEW, split_axis=1, concat_axis=0, tiled=True)
    in_half, views = lax.optimization_barrier((in_half, views))
    swap = [(0, 1), (1, 0)]
    in_other = lax.ppermute(in_half, "core", swap)
    flat_block = views.reshape(-1, width_out)
    block_mine = lax.dynamic_slice_in_dim(flat_block, core * half_in, half_in, axis=1)
    block_other = lax.dynamic_slice_in_dim(flat_block, (1 - core) * half_in, half_in, axis=1)
    triple_in = jnp.einsum(
        "pc,jmcd->mpjd", block_mine, in_half, preferred_element_type=jnp.float32
    ) + jnp.einsum(
        "pc,jmcd->mpjd", block_other, in_other, preferred_element_type=jnp.float32
    )
    triple_in = triple_in.astype(jnp.bfloat16).reshape((3,) + views.shape)
    mixed = send_back(attend(triple_in[0], triple_in[1], triple_in[2], head_scale))
    out_half, mixed = lax.optimization_barrier((out_half, mixed))
    out_other = lax.ppermute(out_half, "core", swap)
    mixed = jnp.moveaxis(
        mixed.reshape(local_views, samples, local_rows, local_cols, width_out), 0, 1
    )
    flat_mixed = mixed.reshape(-1, width_out)
    cols_mine = jnp.dot(flat_mixed, out_half, preferred_element_type=jnp.float32)
    cols_other = jnp.dot(flat_mixed, out_other, preferred_element_type=jnp.float32)
    projected = jnp.where(
        core == 0,
        jnp.concatenate([cols_mine, cols_other], axis=1),
        jnp.concatenate([cols_other, cols_mine], axis=1),
    )
    return (resid_float + projected.reshape(resid_float.shape)).astype(jnp.bfloat16)

ROW = ("chip", "core")
VIEW = ("vz", "vy")


def solution(mesh):
    cores = 2
    split = jax.sharding.Mesh(
        mesh.devices.reshape(
            mesh.shape["view"] // 2, 2, mesh.shape["row"] // cores, cores
        ),
        ("vz", "vy", "chip", "core"),
    )
    placed = (
        P(None, VIEW, ROW, None, None),
        P(),
        P(),
        P(None, VIEW),
        P(),
        P(),
        P(),
        P(None, None, None, ROW),
        P(),
        P(),
        P(None, None, VIEW),
        P(VIEW, None),
        P(),
    )
    return jax.shard_map(
        local,
        mesh=split,
        in_specs=placed,
        out_specs=P(None, VIEW, ROW, None, None),
        check_vma=False,
    )
```

```python
import math

import jax
import jax.numpy as jnp
from jax import lax
from jax.sharding import PartitionSpec as P

GROUPS = 32


epsilon = 1e-05


def attend(query, key_block, value, head_scale):
    view_count = query.shape[0]
    item_count = query.shape[2]
    channels = query.shape[3]
    head_count = head_scale.shape[0]
    head_size = channels // head_count
    query_heads = query.reshape(view_count, item_count, head_count, head_size)
    key_heads = key_block.reshape(view_count, item_count, head_count, head_size)
    value_heads = value.reshape(view_count, item_count, head_count, head_size)
    scores = jnp.einsum(
        "vihd,uihd->ihvu", query_heads, key_heads, preferred_element_type=jnp.float32
    )
    scores = scores * (head_scale / math.sqrt(head_size))[None, :, None, None]
    peak_score = jnp.max(scores, axis=-1, keepdims=True)
    exp_scores = jnp.exp(scores - peak_score)
    soft_weights = (exp_scores / jnp.sum(exp_scores, axis=-1, keepdims=True)).astype(jnp.bfloat16)
    mixed = jnp.einsum(
        "ihvu,uihd->vihd", soft_weights, value_heads, preferred_element_type=jnp.float32
    )
    return mixed.astype(jnp.bfloat16).reshape(view_count, 1, item_count, channels)


def send_back(mixed):
    return lax.all_to_all(mixed, VIEW, split_axis=0, concat_axis=1, tiled=True)


def local(
    latent,
    gn_gain,
    gn_bias,
    cam_idx,
    noise_idx,
    cam_table,
    noise_table,
    conv_w,
    conv_bias,
    ln_gain,
    attn_in,
    attn_out,
    head_scale,
):
    samples, local_views, local_rows, local_cols, channels = latent.shape
    width_out = ln_gain.shape[0]
    out_part = conv_w.shape[-1]
    core = lax.axis_index("core")
    swap = [(0, 1), (1, 0)]
    rows_mine = lax.all_gather(latent, "chip", axis=2, tiled=False)
    rows_mine, attn_in = lax.optimization_barrier((rows_mine, attn_in))
    rows_other = lax.ppermute(rows_mine, "core", swap)
    whole = jnp.where(
        core == 0,
        jnp.stack([rows_mine, rows_other], axis=3),
        jnp.stack([rows_other, rows_mine], axis=3),
    )
    whole = whole.reshape(samples, local_views, -1, local_cols, channels)
    half_in = attn_in.shape[1] // 2
    half_out = attn_out.shape[1] // 2
    in_half = lax.dynamic_slice_in_dim(attn_in, core * half_in, half_in, axis=1)
    in_half = lax.all_gather(in_half, VIEW, axis=0, tiled=False)
    out_half = lax.dynamic_slice_in_dim(attn_out, core * half_out, half_out, axis=1)
    view_devices = lax.axis_size(VIEW)
    out_half = jnp.broadcast_to(out_half[None], (view_devices,) + out_half.shape)
    out_half = lax.all_to_all(out_half, VIEW, split_axis=0, concat_axis=0, tiled=True)
    out_half = out_half.reshape(-1, half_out)

    all_rows = whole.shape[2]
    x_float = whole.astype(jnp.float32)
    grouped = x_float.reshape(
        samples, local_views, all_rows, local_cols, GROUPS, channels // GROUPS
    )
    average = jnp.mean(grouped, axis=(2, 3, 5), keepdims=True)
    centred = grouped - average
    variance = jnp.mean(centred * centred, axis=(2, 3, 5), keepdims=True)
    normed = (centred * lax.rsqrt(variance + epsilon)).reshape(x_float.shape)
    cam_hot = (cam_idx[:, :, None] == jnp.arange(cam_table.shape[0], dtype=jnp.int32)).astype(
        jnp.bfloat16
    )
    cam_film = jnp.einsum("svn,nc->svc", cam_hot, cam_table, preferred_element_type=jnp.float32)
    noise_hot = (noise_idx[:, None] == jnp.arange(noise_table.shape[0], dtype=jnp.int32)).astype(
        jnp.bfloat16
    )
    noise_film = jnp.dot(noise_hot, noise_table, preferred_element_type=jnp.float32)
    film_rows = cam_film + noise_film[:, None, :]
    film_scale = film_rows[:, :, None, None, :channels]
    film_shift = film_rows[:, :, None, None, channels:]
    hidden = (normed * gn_gain + gn_bias) * (1.0 + film_scale) + film_shift
    activated = jax.nn.silu(hidden).astype(jnp.bfloat16)
    out_half, activated = lax.optimization_barrier((out_half, activated))
    conv_out = lax.conv_general_dilated(
        activated.reshape(samples * local_views, all_rows, local_cols, channels),
        conv_w,
        window_strides=(1, 1),
        padding=((1, 1), (1, 1)),
        dimension_numbers=("NHWC", "HWIO", "NHWC"),
        preferred_element_type=jnp.float32,
    ).reshape(samples, local_views, all_rows, local_cols, out_part)
    me = lax.axis_index("chip") * lax.axis_size("core") + core
    bias_part = lax.dynamic_slice_in_dim(conv_bias, me * out_part, out_part)
    latent_part = lax.dynamic_slice_in_dim(whole, me * out_part, out_part, axis=4)
    resid_part = (latent_part.astype(jnp.float32) + conv_out + bias_part).astype(jnp.bfloat16)
    resid_out = lax.all_to_all(resid_part, ROW, split_axis=2, concat_axis=4, tiled=True)
    resid_float = resid_out.astype(jnp.float32)
    middle = jnp.mean(resid_float, axis=-1, keepdims=True)
    spread_y = jnp.mean((resid_float - middle) ** 2, axis=-1, keepdims=True)
    normed_y = ((resid_float - middle) * lax.rsqrt(spread_y + epsilon) * ln_gain).astype(
        jnp.bfloat16
    )
    view_devices = lax.axis_size(VIEW)
    per_device = samples * local_rows * local_cols // view_devices
    pixel_major = jnp.moveaxis(normed_y, 1, 0).reshape(
        local_views, view_devices, per_device, width_out
    )
    views = lax.all_to_all(pixel_major, VIEW, split_axis=1, concat_axis=0, tiled=True)
    in_half, views = lax.optimization_barrier((in_half, views))
    in_other = lax.ppermute(in_half, "core", swap)
    flat_block = views.reshape(-1, width_out)
    block_mine = lax.dynamic_slice_in_dim(flat_block, core * half_in, half_in, axis=1)
    block_other = lax.dynamic_slice_in_dim(flat_block, (1 - core) * half_in, half_in, axis=1)
    triple_in = jnp.einsum(
        "pc,jmcd->mpjd", block_mine, in_half, preferred_element_type=jnp.float32
    ) + jnp.einsum(
        "pc,jmcd->mpjd", block_other, in_other, preferred_element_type=jnp.float32
    )
    triple_in = triple_in.astype(jnp.bfloat16).reshape((3,) + views.shape)
    mixed = send_back(attend(triple_in[0], triple_in[1], triple_in[2], head_scale))
    out_half, mixed = lax.optimization_barrier((out_half, mixed))
    out_other = lax.ppermute(out_half, "core", swap)
    mixed = jnp.moveaxis(
        mixed.reshape(local_views, samples, local_rows, local_cols, width_out), 0, 1
    )
    flat_mixed = mixed.reshape(-1, width_out)
    cols_mine = jnp.dot(flat_mixed, out_half, preferred_element_type=jnp.float32)
    cols_other = jnp.dot(flat_mixed, out_other, preferred_element_type=jnp.float32)
    projected = jnp.where(
        core == 0,
        jnp.concatenate([cols_mine, cols_other], axis=1),
        jnp.concatenate([cols_other, cols_mine], axis=1),
    )
    return (resid_float + projected.reshape(resid_float.shape)).astype(jnp.bfloat16)

ROW = ("chip", "core")
VIEW = ("vz", "vy")


def solution(mesh):
    cores = 2
    split = jax.sharding.Mesh(
        mesh.devices.reshape(
            mesh.shape["view"] // 2, 2, mesh.shape["row"] // cores, cores
        ),
        ("vz", "vy", "chip", "core"),
    )
    placed = (
        P(None, VIEW, ROW, None, None),
        P(),
        P(),
        P(None, VIEW),
        P(),
        P(),
        P(),
        P(None, None, None, ROW),
        P(),
        P(),
        P(None, None, VIEW),
        P(VIEW, None),
        P(),
    )
    return jax.shard_map(
        local,
        mesh=split,
        in_specs=placed,
        out_specs=P(None, VIEW, ROW, None, None),
        check_vma=False,
    )
```

```python
import math

import jax
import jax.numpy as jnp
from jax import lax
from jax.sharding import PartitionSpec as P

GROUPS = 32


epsilon = 1e-05


def attend(query, key_block, value, head_scale):
    view_count = query.shape[0]
    item_count = query.shape[2]
    channels = query.shape[3]
    head_count = head_scale.shape[0]
    head_size = channels // head_count
    query_heads = query.reshape(view_count, item_count, head_count, head_size)
    key_heads = key_block.reshape(view_count, item_count, head_count, head_size)
    value_heads = value.reshape(view_count, item_count, head_count, head_size)
    scores = jnp.einsum(
        "vihd,uihd->ihvu", query_heads, key_heads, preferred_element_type=jnp.float32
    )
    scores = scores * (head_scale / math.sqrt(head_size))[None, :, None, None]
    peak_score = jnp.max(scores, axis=-1, keepdims=True)
    exp_scores = jnp.exp(scores - peak_score)
    soft_weights = (exp_scores / jnp.sum(exp_scores, axis=-1, keepdims=True)).astype(jnp.bfloat16)
    mixed = jnp.einsum(
        "ihvu,uihd->vihd", soft_weights, value_heads, preferred_element_type=jnp.float32
    )
    return mixed.astype(jnp.bfloat16).reshape(view_count, 1, item_count, channels)


def send_back(mixed):
    return lax.all_to_all(mixed, VIEW, split_axis=0, concat_axis=1, tiled=True)


def local(
    latent,
    gn_gain,
    gn_bias,
    cam_idx,
    noise_idx,
    cam_table,
    noise_table,
    conv_w,
    conv_bias,
    ln_gain,
    attn_in,
    attn_out,
    head_scale,
):
    samples, local_views, local_rows, local_cols, channels = latent.shape
    width_out = ln_gain.shape[0]
    out_part = conv_w.shape[-1]
    whole = lax.all_gather(latent, ROW, axis=2, tiled=True)
    whole, attn_in = lax.optimization_barrier((whole, attn_in))
    core = lax.axis_index("core")
    half_in = attn_in.shape[1] // 2
    half_out = attn_out.shape[1] // 2
    in_half = lax.dynamic_slice_in_dim(attn_in, core * half_in, half_in, axis=1)
    in_half = lax.all_gather(in_half, VIEW, axis=0, tiled=False)
    out_half = lax.dynamic_slice_in_dim(attn_out, core * half_out, half_out, axis=1)
    view_devices = lax.axis_size(VIEW)
    out_half = jnp.broadcast_to(out_half[None], (view_devices,) + out_half.shape)
    out_half = lax.all_to_all(out_half, VIEW, split_axis=0, concat_axis=0, tiled=True)
    out_half = out_half.reshape(-1, half_out)

    all_rows = whole.shape[2]
    x_float = whole.astype(jnp.float32)
    grouped = x_float.reshape(
        samples, local_views, all_rows, local_cols, GROUPS, channels // GROUPS
    )
    average = jnp.mean(grouped, axis=(2, 3, 5), keepdims=True)
    centred = grouped - average
    variance = jnp.mean(centred * centred, axis=(2, 3, 5), keepdims=True)
    normed = (centred * lax.rsqrt(variance + epsilon)).reshape(x_float.shape)
    cam_film = jnp.take(cam_table, cam_idx, axis=0).astype(jnp.float32)
    noise_film = jnp.take(noise_table, noise_idx, axis=0).astype(jnp.float32)
    film_rows = cam_film + noise_film[:, None, :]
    film_scale = film_rows[:, :, None, None, :channels]
    film_shift = film_rows[:, :, None, None, channels:]
    hidden = (normed * gn_gain + gn_bias) * (1.0 + film_scale) + film_shift
    activated = jax.nn.silu(hidden).astype(jnp.bfloat16)
    out_half, activated = lax.optimization_barrier((out_half, activated))
    taps = conv_w.shape[1]
    padded = jnp.pad(activated, ((0, 0), (0, 0), (1, 1), (0, 0), (0, 0)))
    tap_sum = None
    for tap_row in range(conv_w.shape[0]):
        rows_in = padded[:, :, tap_row : tap_row + all_rows].reshape(-1, channels)
        weight_row = jnp.transpose(conv_w[tap_row], (1, 0, 2)).reshape(channels, taps * out_part)
        part = jnp.dot(rows_in, weight_row, preferred_element_type=jnp.float32)
        tap_sum = part if tap_sum is None else tap_sum + part
    tap_sum = tap_sum.reshape(samples, local_views, all_rows, local_cols, taps, out_part)
    wide = jnp.pad(tap_sum, ((0, 0), (0, 0), (0, 0), (1, 1), (0, 0), (0, 0)))
    conv_out = (
        wide[:, :, :, 0:local_cols, 0]
        + wide[:, :, :, 1 : local_cols + 1, 1]
        + wide[:, :, :, 2 : local_cols + 2, 2]
    )
    me = lax.axis_index("chip") * lax.axis_size("core") + core
    bias_part = lax.dynamic_slice_in_dim(conv_bias, me * out_part, out_part)
    latent_part = lax.dynamic_slice_in_dim(whole, me * out_part, out_part, axis=4)
    resid_part = (latent_part.astype(jnp.float32) + conv_out + bias_part).astype(jnp.bfloat16)
    resid_out = lax.all_to_all(resid_part, ROW, split_axis=2, concat_axis=4, tiled=True)
    resid_float = resid_out.astype(jnp.float32)
    middle = jnp.mean(resid_float, axis=-1, keepdims=True)
    spread_y = jnp.mean((resid_float - middle) ** 2, axis=-1, keepdims=True)
    normed_y = ((resid_float - middle) * lax.rsqrt(spread_y + epsilon) * ln_gain).astype(
        jnp.bfloat16
    )
    view_devices = lax.axis_size(VIEW)
    per_device = samples * local_rows * local_cols // view_devices
    pixel_major = jnp.moveaxis(normed_y, 1, 0).reshape(
        local_views, view_devices, per_device, width_out
    )
    views = lax.all_to_all(pixel_major, VIEW, split_axis=1, concat_axis=0, tiled=True)
    in_half, views = lax.optimization_barrier((in_half, views))
    swap = [(0, 1), (1, 0)]
    in_other = lax.ppermute(in_half, "core", swap)
    flat_block = views.reshape(-1, width_out)
    block_mine = lax.dynamic_slice_in_dim(flat_block, core * half_in, half_in, axis=1)
    block_other = lax.dynamic_slice_in_dim(flat_block, (1 - core) * half_in, half_in, axis=1)
    triple_in = jnp.einsum(
        "pc,jmcd->mpjd", block_mine, in_half, preferred_element_type=jnp.float32
    ) + jnp.einsum(
        "pc,jmcd->mpjd", block_other, in_other, preferred_element_type=jnp.float32
    )
    triple_in = triple_in.astype(jnp.bfloat16).reshape((3,) + views.shape)
    mixed = send_back(attend(triple_in[0], triple_in[1], triple_in[2], head_scale))
    out_half, mixed = lax.optimization_barrier((out_half, mixed))
    out_other = lax.ppermute(out_half, "core", swap)
    mixed = jnp.moveaxis(
        mixed.reshape(local_views, samples, local_rows, local_cols, width_out), 0, 1
    )
    flat_mixed = mixed.reshape(-1, width_out)
    cols_mine = jnp.dot(flat_mixed, out_half, preferred_element_type=jnp.float32)
    cols_other = jnp.dot(flat_mixed, out_other, preferred_element_type=jnp.float32)
    projected = jnp.where(
        core == 0,
        jnp.concatenate([cols_mine, cols_other], axis=1),
        jnp.concatenate([cols_other, cols_mine], axis=1),
    )
    return (resid_float + projected.reshape(resid_float.shape)).astype(jnp.bfloat16)

ROW = ("chip", "core")
VIEW = ("vz", "vy")


def solution(mesh):
    cores = 2
    split = jax.sharding.Mesh(
        mesh.devices.reshape(
            mesh.shape["view"] // 2, 2, mesh.shape["row"] // cores, cores
        ),
        ("vz", "vy", "chip", "core"),
    )
    placed = (
        P(None, VIEW, ROW, None, None),
        P(),
        P(),
        P(None, VIEW),
        P(),
        P(),
        P(),
        P(None, None, None, ROW),
        P(),
        P(),
        P(None, None, VIEW),
        P(VIEW, None),
        P(),
    )
    return jax.shard_map(
        local,
        mesh=split,
        in_specs=placed,
        out_specs=P(None, VIEW, ROW, None, None),
        check_vma=False,
    )
```

```python
import math

import jax
import jax.numpy as jnp
from jax import lax
from jax.sharding import PartitionSpec as P

GROUPS = 32


epsilon = 1e-05


def attend(query, key_block, value, head_scale):
    view_count = query.shape[0]
    item_count = query.shape[2]
    channels = query.shape[3]
    head_count = head_scale.shape[0]
    head_size = channels // head_count
    query_heads = query.reshape(view_count, item_count, head_count, head_size)
    key_heads = key_block.reshape(view_count, item_count, head_count, head_size)
    value_heads = value.reshape(view_count, item_count, head_count, head_size)
    scores = jnp.einsum(
        "vihd,uihd->ihvu", query_heads, key_heads, preferred_element_type=jnp.float32
    )
    scores = scores * (head_scale / math.sqrt(head_size))[None, :, None, None]
    peak_score = jnp.max(scores, axis=-1, keepdims=True)
    exp_scores = jnp.exp(scores - peak_score)
    soft_weights = (exp_scores / jnp.sum(exp_scores, axis=-1, keepdims=True)).astype(jnp.bfloat16)
    mixed = jnp.einsum(
        "ihvu,uihd->vihd", soft_weights, value_heads, preferred_element_type=jnp.float32
    )
    return mixed.astype(jnp.bfloat16).reshape(view_count, 1, item_count, channels)


def send_back(mixed):
    return lax.all_to_all(mixed, VIEW, split_axis=0, concat_axis=1, tiled=True)


def local(
    latent,
    gn_gain,
    gn_bias,
    cam_idx,
    noise_idx,
    cam_table,
    noise_table,
    conv_w,
    conv_bias,
    ln_gain,
    attn_in,
    attn_out,
    head_scale,
):
    samples, local_views, local_rows, local_cols, channels = latent.shape
    width_out = ln_gain.shape[0]
    out_part = conv_w.shape[-1]
    whole = lax.all_gather(latent, ROW, axis=2, tiled=True)
    whole, attn_in = lax.optimization_barrier((whole, attn_in))
    core = lax.axis_index("core")
    half_in = attn_in.shape[1] // 2
    half_out = attn_out.shape[1] // 2
    in_half = lax.dynamic_slice_in_dim(attn_in, core * half_in, half_in, axis=1)
    in_half = lax.all_gather(in_half, VIEW, axis=0, tiled=False)
    out_half = lax.dynamic_slice_in_dim(attn_out, core * half_out, half_out, axis=1)
    view_devices = lax.axis_size(VIEW)
    out_half = jnp.broadcast_to(out_half[None], (view_devices,) + out_half.shape)
    out_half = lax.all_to_all(out_half, VIEW, split_axis=0, concat_axis=0, tiled=True)
    out_half = out_half.reshape(-1, half_out)

    all_rows = whole.shape[2]
    x_float = whole.astype(jnp.float32)
    grouped = x_float.reshape(
        samples, local_views, all_rows, local_cols, GROUPS, channels // GROUPS
    )
    average = jnp.mean(grouped, axis=(2, 3, 5), keepdims=True)
    centred = grouped - average
    variance = jnp.mean(centred * centred, axis=(2, 3, 5), keepdims=True)
    normed = (centred * lax.rsqrt(variance + epsilon)).reshape(x_float.shape)
    cam_film = jnp.take(cam_table, cam_idx, axis=0).astype(jnp.float32)
    noise_film = jnp.take(noise_table, noise_idx, axis=0).astype(jnp.float32)
    film_rows = cam_film + noise_film[:, None, :]
    film_scale = film_rows[:, :, None, None, :channels]
    film_shift = film_rows[:, :, None, None, channels:]
    hidden = (normed * gn_gain + gn_bias) * (1.0 + film_scale) + film_shift
    activated = jax.nn.silu(hidden).astype(jnp.bfloat16)
    out_half, activated = lax.optimization_barrier((out_half, activated))
    taps = conv_w.shape[1]
    padded = jnp.pad(activated, ((0, 0), (0, 0), (1, 1), (0, 0), (0, 0)))
    tap_sum = None
    for tap_row in range(conv_w.shape[0]):
        rows_in = padded[:, :, tap_row : tap_row + all_rows].reshape(-1, channels)
        weight_row = jnp.transpose(conv_w[tap_row], (1, 0, 2)).reshape(channels, taps * out_part)
        part = jnp.dot(rows_in, weight_row, preferred_element_type=jnp.float32)
        tap_sum = part if tap_sum is None else tap_sum + part
    tap_sum = tap_sum.reshape(samples, local_views, all_rows, local_cols, taps, out_part)
    wide = jnp.pad(tap_sum, ((0, 0), (0, 0), (0, 0), (1, 1), (0, 0), (0, 0)))
    conv_out = (
        wide[:, :, :, 0:local_cols, 0]
        + wide[:, :, :, 1 : local_cols + 1, 1]
        + wide[:, :, :, 2 : local_cols + 2, 2]
    )
    me = lax.axis_index("chip") * lax.axis_size("core") + core
    conv_part = conv_out.astype(jnp.bfloat16)
    conv_rows = lax.all_to_all(conv_part, ROW, split_axis=2, concat_axis=4, tiled=True)
    resid_out = (
        latent.astype(jnp.float32) + conv_rows.astype(jnp.float32) + conv_bias
    ).astype(jnp.bfloat16)
    resid_float = resid_out.astype(jnp.float32)
    middle = jnp.mean(resid_float, axis=-1, keepdims=True)
    spread_y = jnp.mean((resid_float - middle) ** 2, axis=-1, keepdims=True)
    normed_y = ((resid_float - middle) * lax.rsqrt(spread_y + epsilon) * ln_gain).astype(
        jnp.bfloat16
    )
    view_devices = lax.axis_size(VIEW)
    per_device = samples * local_rows * local_cols // view_devices
    pixel_major = jnp.moveaxis(normed_y, 1, 0).reshape(
        local_views, view_devices, per_device, width_out
    )
    views = lax.all_to_all(pixel_major, VIEW, split_axis=1, concat_axis=0, tiled=True)
    in_half, views = lax.optimization_barrier((in_half, views))
    swap = [(0, 1), (1, 0)]
    in_other = lax.ppermute(in_half, "core", swap)
    flat_block = views.reshape(-1, width_out)
    block_mine = lax.dynamic_slice_in_dim(flat_block, core * half_in, half_in, axis=1)
    block_other = lax.dynamic_slice_in_dim(flat_block, (1 - core) * half_in, half_in, axis=1)
    triple_in = jnp.einsum(
        "pc,jmcd->mpjd", block_mine, in_half, preferred_element_type=jnp.float32
    ) + jnp.einsum(
        "pc,jmcd->mpjd", block_other, in_other, preferred_element_type=jnp.float32
    )
    triple_in = triple_in.astype(jnp.bfloat16).reshape((3,) + views.shape)
    mixed = send_back(attend(triple_in[0], triple_in[1], triple_in[2], head_scale))
    out_half, mixed = lax.optimization_barrier((out_half, mixed))
    out_other = lax.ppermute(out_half, "core", swap)
    mixed = jnp.moveaxis(
        mixed.reshape(local_views, samples, local_rows, local_cols, width_out), 0, 1
    )
    flat_mixed = mixed.reshape(-1, width_out)
    cols_mine = jnp.dot(flat_mixed, out_half, preferred_element_type=jnp.float32)
    cols_other = jnp.dot(flat_mixed, out_other, preferred_element_type=jnp.float32)
    projected = jnp.where(
        core == 0,
        jnp.concatenate([cols_mine, cols_other], axis=1),
        jnp.concatenate([cols_other, cols_mine], axis=1),
    )
    return (resid_float + projected.reshape(resid_float.shape)).astype(jnp.bfloat16)

ROW = ("chip", "core")
VIEW = ("vz", "vy")


def solution(mesh):
    cores = 2
    split = jax.sharding.Mesh(
        mesh.devices.reshape(
            mesh.shape["view"] // 2, 2, mesh.shape["row"] // cores, cores
        ),
        ("vz", "vy", "chip", "core"),
    )
    placed = (
        P(None, VIEW, ROW, None, None),
        P(),
        P(),
        P(None, VIEW),
        P(),
        P(),
        P(),
        P(None, None, None, ROW),
        P(),
        P(),
        P(None, None, VIEW),
        P(VIEW, None),
        P(),
    )
    return jax.shard_map(
        local,
        mesh=split,
        in_specs=placed,
        out_specs=P(None, VIEW, ROW, None, None),
        check_vma=False,
    )
```

```python
import math

import jax
import jax.numpy as jnp
from jax import lax
from jax.sharding import PartitionSpec as P

GROUPS = 32


epsilon = 1e-05


def attend(query, key_block, value, head_scale):
    view_count = query.shape[0]
    item_count = query.shape[2]
    channels = query.shape[3]
    head_count = head_scale.shape[0]
    head_size = channels // head_count
    query_heads = query.reshape(view_count, item_count, head_count, head_size)
    key_heads = key_block.reshape(view_count, item_count, head_count, head_size)
    value_heads = value.reshape(view_count, item_count, head_count, head_size)
    scores = jnp.einsum(
        "vihd,uihd->ihvu", query_heads, key_heads, preferred_element_type=jnp.float32
    )
    scores = scores * (head_scale / math.sqrt(head_size))[None, :, None, None]
    peak_score = jnp.max(scores, axis=-1, keepdims=True)
    exp_scores = jnp.exp(scores - peak_score)
    soft_weights = (exp_scores / jnp.sum(exp_scores, axis=-1, keepdims=True)).astype(jnp.bfloat16)
    mixed = jnp.einsum(
        "ihvu,uihd->vihd", soft_weights, value_heads, preferred_element_type=jnp.float32
    )
    return mixed.astype(jnp.bfloat16).reshape(view_count, 1, item_count, channels)


def send_back(mixed):
    ys = lax.axis_size("vy")
    zs = lax.axis_size("vz")
    parts = mixed.reshape((zs, ys) + mixed.shape[1:])
    parts = lax.all_to_all(parts, "vy", split_axis=1, concat_axis=1, tiled=True)
    parts = lax.all_to_all(parts, "vz", split_axis=0, concat_axis=0, tiled=True)
    return jnp.moveaxis(parts.reshape(mixed.shape), 0, 1)


def send_out(pixel_major):
    ys = lax.axis_size("vy")
    zs = lax.axis_size("vz")
    local_views = pixel_major.shape[0]
    parts = pixel_major.reshape((local_views, zs, ys) + pixel_major.shape[2:])
    parts = lax.all_to_all(parts, "vy", split_axis=2, concat_axis=0, tiled=True)
    parts = lax.all_to_all(parts, "vz", split_axis=1, concat_axis=1, tiled=True)
    parts = jnp.swapaxes(parts, 0, 1)
    return parts.reshape((zs * ys * local_views, 1) + pixel_major.shape[2:])


def local(
    latent,
    gn_gain,
    gn_bias,
    cam_idx,
    noise_idx,
    cam_table,
    noise_table,
    conv_w,
    conv_bias,
    ln_gain,
    attn_in,
    attn_out,
    head_scale,
):
    samples, local_views, local_rows, local_cols, channels = latent.shape
    width_out = ln_gain.shape[0]
    out_part = conv_w.shape[-1]
    whole = lax.all_gather(latent, ROW, axis=2, tiled=True)
    whole, attn_in = lax.optimization_barrier((whole, attn_in))
    core = lax.axis_index("core")
    half_in = attn_in.shape[1] // 2
    half_out = attn_out.shape[1] // 2
    in_half = lax.dynamic_slice_in_dim(attn_in, core * half_in, half_in, axis=1)
    in_half = lax.all_gather(in_half, VIEW, axis=0, tiled=False)
    out_half = lax.dynamic_slice_in_dim(attn_out, core * half_out, half_out, axis=1)
    view_devices = lax.axis_size(VIEW)
    out_half = jnp.broadcast_to(out_half[None], (view_devices,) + out_half.shape)
    out_half = lax.all_to_all(out_half, VIEW, split_axis=0, concat_axis=0, tiled=True)
    out_half = out_half.reshape(-1, half_out)

    all_rows = whole.shape[2]
    x_float = whole.astype(jnp.float32)
    grouped = x_float.reshape(
        samples, local_views, all_rows, local_cols, GROUPS, channels // GROUPS
    )
    average = jnp.mean(grouped, axis=(2, 3, 5), keepdims=True)
    centred = grouped - average
    variance = jnp.mean(centred * centred, axis=(2, 3, 5), keepdims=True)
    normed = (centred * lax.rsqrt(variance + epsilon)).reshape(x_float.shape)
    cam_film = jnp.take(cam_table, cam_idx, axis=0).astype(jnp.float32)
    noise_film = jnp.take(noise_table, noise_idx, axis=0).astype(jnp.float32)
    film_rows = cam_film + noise_film[:, None, :]
    film_scale = film_rows[:, :, None, None, :channels]
    film_shift = film_rows[:, :, None, None, channels:]
    hidden = (normed * gn_gain + gn_bias) * (1.0 + film_scale) + film_shift
    activated = jax.nn.silu(hidden).astype(jnp.bfloat16)
    out_half, activated = lax.optimization_barrier((out_half, activated))
    taps = conv_w.shape[1]
    padded = jnp.pad(activated, ((0, 0), (0, 0), (1, 1), (0, 0), (0, 0)))
    tap_sum = None
    for tap_row in range(conv_w.shape[0]):
        rows_in = padded[:, :, tap_row : tap_row + all_rows].reshape(-1, channels)
        weight_row = jnp.transpose(conv_w[tap_row], (1, 0, 2)).reshape(channels, taps * out_part)
        part = jnp.dot(rows_in, weight_row, preferred_element_type=jnp.float32)
        tap_sum = part if tap_sum is None else tap_sum + part
    tap_sum = tap_sum.reshape(samples, local_views, all_rows, local_cols, taps, out_part)
    wide = jnp.pad(tap_sum, ((0, 0), (0, 0), (0, 0), (1, 1), (0, 0), (0, 0)))
    conv_out = (
        wide[:, :, :, 0:local_cols, 0]
        + wide[:, :, :, 1 : local_cols + 1, 1]
        + wide[:, :, :, 2 : local_cols + 2, 2]
    )
    me = lax.axis_index("chip") * lax.axis_size("core") + core
    conv_part = conv_out.astype(jnp.bfloat16)
    conv_rows = lax.all_to_all(conv_part, ROW, split_axis=2, concat_axis=4, tiled=True)
    resid_out = (
        latent.astype(jnp.float32) + conv_rows.astype(jnp.float32) + conv_bias
    ).astype(jnp.bfloat16)
    resid_float = resid_out.astype(jnp.float32)
    middle = jnp.mean(resid_float, axis=-1, keepdims=True)
    spread_y = jnp.mean((resid_float - middle) ** 2, axis=-1, keepdims=True)
    normed_y = ((resid_float - middle) * lax.rsqrt(spread_y + epsilon) * ln_gain).astype(
        jnp.bfloat16
    )
    view_devices = lax.axis_size(VIEW)
    per_device = samples * local_rows * local_cols // view_devices
    pixel_major = jnp.moveaxis(normed_y, 1, 0).reshape(
        local_views, view_devices, per_device, width_out
    )
    views = send_out(pixel_major)
    in_half, views = lax.optimization_barrier((in_half, views))
    swap = [(0, 1), (1, 0)]
    in_other = lax.ppermute(in_half, "core", swap)
    flat_block = views.reshape(-1, width_out)
    block_mine = lax.dynamic_slice_in_dim(flat_block, core * half_in, half_in, axis=1)
    block_other = lax.dynamic_slice_in_dim(flat_block, (1 - core) * half_in, half_in, axis=1)
    triple_in = jnp.einsum(
        "pc,jmcd->mpjd", block_mine, in_half, preferred_element_type=jnp.float32
    ) + jnp.einsum(
        "pc,jmcd->mpjd", block_other, in_other, preferred_element_type=jnp.float32
    )
    triple_in = triple_in.astype(jnp.bfloat16).reshape((3,) + views.shape)
    mixed = send_back(attend(triple_in[0], triple_in[1], triple_in[2], head_scale))
    out_half, mixed = lax.optimization_barrier((out_half, mixed))
    out_other = lax.ppermute(out_half, "core", swap)
    mixed = jnp.moveaxis(
        mixed.reshape(local_views, samples, local_rows, local_cols, width_out), 0, 1
    )
    flat_mixed = mixed.reshape(-1, width_out)
    cols_mine = jnp.dot(flat_mixed, out_half, preferred_element_type=jnp.float32)
    cols_other = jnp.dot(flat_mixed, out_other, preferred_element_type=jnp.float32)
    projected = jnp.where(
        core == 0,
        jnp.concatenate([cols_mine, cols_other], axis=1),
        jnp.concatenate([cols_other, cols_mine], axis=1),
    )
    return (resid_float + projected.reshape(resid_float.shape)).astype(jnp.bfloat16)

ROW = ("chip", "core")
VIEW = ("vz", "vy")


def solution(mesh):
    cores = 2
    split = jax.sharding.Mesh(
        mesh.devices.reshape(
            mesh.shape["view"] // 2, 2, mesh.shape["row"] // cores, cores
        ),
        ("vz", "vy", "chip", "core"),
    )
    placed = (
        P(None, VIEW, ROW, None, None),
        P(),
        P(),
        P(None, VIEW),
        P(),
        P(),
        P(),
        P(None, None, None, ROW),
        P(),
        P(),
        P(None, None, VIEW),
        P(VIEW, None),
        P(),
    )
    return jax.shard_map(
        local,
        mesh=split,
        in_specs=placed,
        out_specs=P(None, VIEW, ROW, None, None),
        check_vma=False,
    )
```

```python
import math

import jax
import jax.numpy as jnp
from jax import lax
from jax.sharding import PartitionSpec as P

GROUPS = 32


epsilon = 1e-05


def attend(query, key_block, value, head_scale):
    view_count = query.shape[0]
    item_count = query.shape[2]
    channels = query.shape[3]
    head_count = head_scale.shape[0]
    head_size = channels // head_count
    query_heads = query.reshape(view_count, item_count, head_count, head_size)
    key_heads = key_block.reshape(view_count, item_count, head_count, head_size)
    value_heads = value.reshape(view_count, item_count, head_count, head_size)
    scores = jnp.einsum(
        "vihd,uihd->ihvu", query_heads, key_heads, preferred_element_type=jnp.float32
    )
    scores = scores * (head_scale / math.sqrt(head_size))[None, :, None, None]
    peak_score = jnp.max(scores, axis=-1, keepdims=True)
    exp_scores = jnp.exp(scores - peak_score)
    soft_weights = (exp_scores / jnp.sum(exp_scores, axis=-1, keepdims=True)).astype(jnp.bfloat16)
    mixed = jnp.einsum(
        "ihvu,uihd->vihd", soft_weights, value_heads, preferred_element_type=jnp.float32
    )
    return mixed.astype(jnp.bfloat16).reshape(view_count, 1, item_count, channels)


def send_back(mixed):
    ys = lax.axis_size("vy")
    zs = lax.axis_size("vz")
    parts = mixed.reshape((zs, ys) + mixed.shape[1:])
    parts = lax.all_to_all(parts, "vy", split_axis=1, concat_axis=1, tiled=True)
    parts = lax.all_to_all(parts, "vz", split_axis=0, concat_axis=0, tiled=True)
    return jnp.moveaxis(parts.reshape(mixed.shape), 0, 1)


def send_out(pixel_major):
    ys = lax.axis_size("vy")
    zs = lax.axis_size("vz")
    local_views = pixel_major.shape[0]
    parts = pixel_major.reshape((local_views, zs, ys) + pixel_major.shape[2:])
    parts = lax.all_to_all(parts, "vy", split_axis=2, concat_axis=0, tiled=True)
    parts = lax.all_to_all(parts, "vz", split_axis=1, concat_axis=1, tiled=True)
    parts = jnp.swapaxes(parts, 0, 1)
    return parts.reshape((zs * ys * local_views, 1) + pixel_major.shape[2:])


def local(
    latent,
    gn_gain,
    gn_bias,
    cam_idx,
    noise_idx,
    cam_table,
    noise_table,
    conv_w,
    conv_bias,
    ln_gain,
    attn_in,
    attn_out,
    head_scale,
):
    samples, local_views, local_rows, local_cols, channels = latent.shape
    width_out = ln_gain.shape[0]
    out_part = conv_w.shape[-1]
    whole = lax.all_gather(latent, ROW, axis=2, tiled=True)
    whole, attn_in = lax.optimization_barrier((whole, attn_in))
    core = lax.axis_index("core")
    half_in = attn_in.shape[1] // 2
    half_out = attn_out.shape[1] // 2
    in_half = lax.dynamic_slice_in_dim(attn_in, core * half_in, half_in, axis=1)
    in_half = lax.all_gather(in_half, VIEW, axis=0, tiled=False)
    out_half = lax.dynamic_slice_in_dim(attn_out, core * half_out, half_out, axis=1)
    view_devices = lax.axis_size(VIEW)
    slots = [out_half]
    for shift in range(1, view_devices):
        pairs = [((j + shift) % view_devices, j) for j in range(view_devices)]
        slots.append(lax.ppermute(out_half, VIEW, pairs))
    out_half = jnp.roll(jnp.stack(slots), lax.axis_index(VIEW), axis=0)
    out_half = out_half.reshape(-1, half_out)

    all_rows = whole.shape[2]
    x_float = whole.astype(jnp.float32)
    grouped = x_float.reshape(
        samples, local_views, all_rows, local_cols, GROUPS, channels // GROUPS
    )
    average = jnp.mean(grouped, axis=(2, 3, 5), keepdims=True)
    centred = grouped - average
    variance = jnp.mean(centred * centred, axis=(2, 3, 5), keepdims=True)
    normed = (centred * lax.rsqrt(variance + epsilon)).reshape(x_float.shape)
    cam_film = jnp.take(cam_table, cam_idx, axis=0).astype(jnp.float32)
    noise_film = jnp.take(noise_table, noise_idx, axis=0).astype(jnp.float32)
    film_rows = cam_film + noise_film[:, None, :]
    film_scale = film_rows[:, :, None, None, :channels]
    film_shift = film_rows[:, :, None, None, channels:]
    hidden = (normed * gn_gain + gn_bias) * (1.0 + film_scale) + film_shift
    activated = jax.nn.silu(hidden).astype(jnp.bfloat16)
    out_half, activated = lax.optimization_barrier((out_half, activated))
    taps = conv_w.shape[1]
    padded = jnp.pad(activated, ((0, 0), (0, 0), (1, 1), (0, 0), (0, 0)))
    tap_sum = None
    for tap_row in range(conv_w.shape[0]):
        rows_in = padded[:, :, tap_row : tap_row + all_rows].reshape(-1, channels)
        weight_row = jnp.transpose(conv_w[tap_row], (1, 0, 2)).reshape(channels, taps * out_part)
        part = jnp.dot(rows_in, weight_row, preferred_element_type=jnp.float32)
        tap_sum = part if tap_sum is None else tap_sum + part
    tap_sum = tap_sum.reshape(samples, local_views, all_rows, local_cols, taps, out_part)
    wide = jnp.pad(tap_sum, ((0, 0), (0, 0), (0, 0), (1, 1), (0, 0), (0, 0)))
    conv_out = (
        wide[:, :, :, 0:local_cols, 0]
        + wide[:, :, :, 1 : local_cols + 1, 1]
        + wide[:, :, :, 2 : local_cols + 2, 2]
    )
    me = lax.axis_index("chip") * lax.axis_size("core") + core
    conv_part = conv_out.astype(jnp.bfloat16)
    conv_rows = lax.all_to_all(conv_part, ROW, split_axis=2, concat_axis=4, tiled=True)
    resid_out = (
        latent.astype(jnp.float32) + conv_rows.astype(jnp.float32) + conv_bias
    ).astype(jnp.bfloat16)
    resid_float = resid_out.astype(jnp.float32)
    middle = jnp.mean(resid_float, axis=-1, keepdims=True)
    spread_y = jnp.mean((resid_float - middle) ** 2, axis=-1, keepdims=True)
    normed_y = ((resid_float - middle) * lax.rsqrt(spread_y + epsilon) * ln_gain).astype(
        jnp.bfloat16
    )
    view_devices = lax.axis_size(VIEW)
    per_device = samples * local_rows * local_cols // view_devices
    pixel_major = jnp.moveaxis(normed_y, 1, 0).reshape(
        local_views, view_devices, per_device, width_out
    )
    views = send_out(pixel_major)
    in_half, views = lax.optimization_barrier((in_half, views))
    swap = [(0, 1), (1, 0)]
    in_other = lax.ppermute(in_half, "core", swap)
    flat_block = views.reshape(-1, width_out)
    block_mine = lax.dynamic_slice_in_dim(flat_block, core * half_in, half_in, axis=1)
    block_other = lax.dynamic_slice_in_dim(flat_block, (1 - core) * half_in, half_in, axis=1)
    triple_in = jnp.einsum(
        "pc,jmcd->mpjd", block_mine, in_half, preferred_element_type=jnp.float32
    ) + jnp.einsum(
        "pc,jmcd->mpjd", block_other, in_other, preferred_element_type=jnp.float32
    )
    triple_in = triple_in.astype(jnp.bfloat16).reshape((3,) + views.shape)
    mixed = send_back(attend(triple_in[0], triple_in[1], triple_in[2], head_scale))
    out_half, mixed = lax.optimization_barrier((out_half, mixed))
    out_other = lax.ppermute(out_half, "core", swap)
    mixed = jnp.moveaxis(
        mixed.reshape(local_views, samples, local_rows, local_cols, width_out), 0, 1
    )
    flat_mixed = mixed.reshape(-1, width_out)
    cols_mine = jnp.dot(flat_mixed, out_half, preferred_element_type=jnp.float32)
    cols_other = jnp.dot(flat_mixed, out_other, preferred_element_type=jnp.float32)
    projected = jnp.where(
        core == 0,
        jnp.concatenate([cols_mine, cols_other], axis=1),
        jnp.concatenate([cols_other, cols_mine], axis=1),
    )
    return (resid_float + projected.reshape(resid_float.shape)).astype(jnp.bfloat16)

ROW = ("chip", "core")
VIEW = ("vz", "vy")


def solution(mesh):
    cores = 2
    split = jax.sharding.Mesh(
        mesh.devices.reshape(
            mesh.shape["view"] // 2, 2, mesh.shape["row"] // cores, cores
        ),
        ("vz", "vy", "chip", "core"),
    )
    placed = (
        P(None, VIEW, ROW, None, None),
        P(),
        P(),
        P(None, VIEW),
        P(),
        P(),
        P(),
        P(None, None, None, ROW),
        P(),
        P(),
        P(None, None, VIEW),
        P(VIEW, None),
        P(),
    )
    return jax.shard_map(
        local,
        mesh=split,
        in_specs=placed,
        out_specs=P(None, VIEW, ROW, None, None),
        check_vma=False,
    )
```

```python
import math

import jax
import jax.numpy as jnp
from jax import lax
from jax.sharding import PartitionSpec as P

GROUPS = 32


epsilon = 1e-05


def attend(query, key_block, value, head_scale):
    view_count = query.shape[0]
    item_count = query.shape[2]
    channels = query.shape[3]
    head_count = head_scale.shape[0]
    head_size = channels // head_count
    query_heads = query.reshape(view_count, item_count, head_count, head_size)
    key_heads = key_block.reshape(view_count, item_count, head_count, head_size)
    value_heads = value.reshape(view_count, item_count, head_count, head_size)
    scores = jnp.einsum(
        "vihd,uihd->ihvu", query_heads, key_heads, preferred_element_type=jnp.float32
    )
    scores = scores * (head_scale / math.sqrt(head_size))[None, :, None, None]
    peak_score = jnp.max(scores, axis=-1, keepdims=True)
    exp_scores = jnp.exp(scores - peak_score)
    soft_weights = (exp_scores / jnp.sum(exp_scores, axis=-1, keepdims=True)).astype(jnp.bfloat16)
    mixed = jnp.einsum(
        "ihvu,uihd->vihd", soft_weights, value_heads, preferred_element_type=jnp.float32
    )
    return mixed.astype(jnp.bfloat16).reshape(view_count, 1, item_count, channels)


def send_back(mixed):
    ys = lax.axis_size("vy")
    zs = lax.axis_size("vz")
    parts = mixed.reshape((zs, ys) + mixed.shape[1:])
    parts = lax.all_to_all(parts, "vy", split_axis=1, concat_axis=1, tiled=True)
    parts = lax.all_to_all(parts, "vz", split_axis=0, concat_axis=0, tiled=True)
    return jnp.moveaxis(parts.reshape(mixed.shape), 0, 1)


def send_out(pixel_major):
    ys = lax.axis_size("vy")
    zs = lax.axis_size("vz")
    local_views = pixel_major.shape[0]
    parts = pixel_major.reshape((local_views, zs, ys) + pixel_major.shape[2:])
    parts = lax.all_to_all(parts, "vy", split_axis=2, concat_axis=0, tiled=True)
    parts = lax.all_to_all(parts, "vz", split_axis=1, concat_axis=1, tiled=True)
    parts = jnp.swapaxes(parts, 0, 1)
    return parts.reshape((zs * ys * local_views, 1) + pixel_major.shape[2:])


def local(
    latent,
    gn_gain,
    gn_bias,
    cam_idx,
    noise_idx,
    cam_table,
    noise_table,
    conv_w,
    conv_bias,
    ln_gain,
    attn_in,
    attn_out,
    head_scale,
):
    samples, local_views, local_rows, local_cols, channels = latent.shape
    width_out = ln_gain.shape[0]
    out_part = conv_w.shape[-1]
    whole = lax.all_gather(latent, ROW, axis=2, tiled=True)
    whole, attn_in = lax.optimization_barrier((whole, attn_in))
    core = lax.axis_index("core")
    half_in = attn_in.shape[1] // 2
    half_out = attn_out.shape[1] // 2
    in_half = lax.dynamic_slice_in_dim(attn_in, core * half_in, half_in, axis=1)
    out_half = lax.dynamic_slice_in_dim(attn_out, core * half_out, half_out, axis=1)
    packed = jnp.concatenate([in_half.reshape(-1), out_half.reshape(-1)])
    packed = lax.all_gather(packed, VIEW, axis=0, tiled=False)
    view_devices = lax.axis_size(VIEW)
    out_half = packed[:, in_half.size :].reshape(-1, half_out)
    in_half = packed[:, : in_half.size].reshape((view_devices,) + in_half.shape)

    all_rows = whole.shape[2]
    x_float = whole.astype(jnp.float32)
    grouped = x_float.reshape(
        samples, local_views, all_rows, local_cols, GROUPS, channels // GROUPS
    )
    average = jnp.mean(grouped, axis=(2, 3, 5), keepdims=True)
    centred = grouped - average
    variance = jnp.mean(centred * centred, axis=(2, 3, 5), keepdims=True)
    normed = (centred * lax.rsqrt(variance + epsilon)).reshape(x_float.shape)
    cam_film = jnp.take(cam_table, cam_idx, axis=0).astype(jnp.float32)
    noise_film = jnp.take(noise_table, noise_idx, axis=0).astype(jnp.float32)
    film_rows = cam_film + noise_film[:, None, :]
    film_scale = film_rows[:, :, None, None, :channels]
    film_shift = film_rows[:, :, None, None, channels:]
    hidden = (normed * gn_gain + gn_bias) * (1.0 + film_scale) + film_shift
    activated = jax.nn.silu(hidden).astype(jnp.bfloat16)
    taps = conv_w.shape[1]
    padded = jnp.pad(activated, ((0, 0), (0, 0), (1, 1), (0, 0), (0, 0)))
    tap_sum = None
    for tap_row in range(conv_w.shape[0]):
        rows_in = padded[:, :, tap_row : tap_row + all_rows].reshape(-1, channels)
        weight_row = jnp.transpose(conv_w[tap_row], (1, 0, 2)).reshape(channels, taps * out_part)
        part = jnp.dot(rows_in, weight_row, preferred_element_type=jnp.float32)
        tap_sum = part if tap_sum is None else tap_sum + part
    tap_sum = tap_sum.reshape(samples, local_views, all_rows, local_cols, taps, out_part)
    wide = jnp.pad(tap_sum, ((0, 0), (0, 0), (0, 0), (1, 1), (0, 0), (0, 0)))
    conv_out = (
        wide[:, :, :, 0:local_cols, 0]
        + wide[:, :, :, 1 : local_cols + 1, 1]
        + wide[:, :, :, 2 : local_cols + 2, 2]
    )
    me = lax.axis_index("chip") * lax.axis_size("core") + core
    conv_part = conv_out.astype(jnp.bfloat16)
    conv_rows = lax.all_to_all(conv_part, ROW, split_axis=2, concat_axis=4, tiled=True)
    resid_out = (
        latent.astype(jnp.float32) + conv_rows.astype(jnp.float32) + conv_bias
    ).astype(jnp.bfloat16)
    resid_float = resid_out.astype(jnp.float32)
    middle = jnp.mean(resid_float, axis=-1, keepdims=True)
    spread_y = jnp.mean((resid_float - middle) ** 2, axis=-1, keepdims=True)
    normed_y = ((resid_float - middle) * lax.rsqrt(spread_y + epsilon) * ln_gain).astype(
        jnp.bfloat16
    )
    view_devices = lax.axis_size(VIEW)
    per_device = samples * local_rows * local_cols // view_devices
    pixel_major = jnp.moveaxis(normed_y, 1, 0).reshape(
        local_views, view_devices, per_device, width_out
    )
    views = send_out(pixel_major)
    in_half, views = lax.optimization_barrier((in_half, views))
    swap = [(0, 1), (1, 0)]
    in_other = lax.ppermute(in_half, "core", swap)
    flat_block = views.reshape(-1, width_out)
    block_mine = lax.dynamic_slice_in_dim(flat_block, core * half_in, half_in, axis=1)
    block_other = lax.dynamic_slice_in_dim(flat_block, (1 - core) * half_in, half_in, axis=1)
    triple_in = jnp.einsum(
        "pc,jmcd->mpjd", block_mine, in_half, preferred_element_type=jnp.float32
    ) + jnp.einsum(
        "pc,jmcd->mpjd", block_other, in_other, preferred_element_type=jnp.float32
    )
    triple_in = triple_in.astype(jnp.bfloat16).reshape((3,) + views.shape)
    mixed = send_back(attend(triple_in[0], triple_in[1], triple_in[2], head_scale))
    out_half, mixed = lax.optimization_barrier((out_half, mixed))
    out_other = lax.ppermute(out_half, "core", swap)
    mixed = jnp.moveaxis(
        mixed.reshape(local_views, samples, local_rows, local_cols, width_out), 0, 1
    )
    flat_mixed = mixed.reshape(-1, width_out)
    cols_mine = jnp.dot(flat_mixed, out_half, preferred_element_type=jnp.float32)
    cols_other = jnp.dot(flat_mixed, out_other, preferred_element_type=jnp.float32)
    projected = jnp.where(
        core == 0,
        jnp.concatenate([cols_mine, cols_other], axis=1),
        jnp.concatenate([cols_other, cols_mine], axis=1),
    )
    return (resid_float + projected.reshape(resid_float.shape)).astype(jnp.bfloat16)

ROW = ("chip", "core")
VIEW = ("vz", "vy")


def solution(mesh):
    cores = 2
    split = jax.sharding.Mesh(
        mesh.devices.reshape(
            mesh.shape["view"] // 2, 2, mesh.shape["row"] // cores, cores
        ),
        ("vz", "vy", "chip", "core"),
    )
    placed = (
        P(None, VIEW, ROW, None, None),
        P(),
        P(),
        P(None, VIEW),
        P(),
        P(),
        P(),
        P(None, None, None, ROW),
        P(),
        P(),
        P(None, None, VIEW),
        P(VIEW, None),
        P(),
    )
    return jax.shard_map(
        local,
        mesh=split,
        in_specs=placed,
        out_specs=P(None, VIEW, ROW, None, None),
        check_vma=False,
    )
```

```python
import math

import jax
import jax.numpy as jnp
from jax import lax
from jax.sharding import PartitionSpec as P

GROUPS = 32


epsilon = 1e-05


def attend(query, key_block, value, head_scale):
    view_count = query.shape[0]
    item_count = query.shape[2]
    channels = query.shape[3]
    head_count = head_scale.shape[0]
    head_size = channels // head_count
    query_heads = query.reshape(view_count, item_count, head_count, head_size)
    key_heads = key_block.reshape(view_count, item_count, head_count, head_size)
    value_heads = value.reshape(view_count, item_count, head_count, head_size)
    scores = jnp.einsum(
        "vihd,uihd->ihvu", query_heads, key_heads, preferred_element_type=jnp.float32
    )
    scores = scores * (head_scale / math.sqrt(head_size))[None, :, None, None]
    peak_score = jnp.max(scores, axis=-1, keepdims=True)
    exp_scores = jnp.exp(scores - peak_score)
    soft_weights = (exp_scores / jnp.sum(exp_scores, axis=-1, keepdims=True)).astype(jnp.bfloat16)
    mixed = jnp.einsum(
        "ihvu,uihd->vihd", soft_weights, value_heads, preferred_element_type=jnp.float32
    )
    return mixed.astype(jnp.bfloat16).reshape(view_count, 1, item_count, channels)


def send_back(mixed):
    return lax.all_to_all(mixed, VIEW, split_axis=0, concat_axis=1, tiled=True)


def send_out(pixel_major):
    ys = lax.axis_size("vy")
    zs = lax.axis_size("vz")
    local_views = pixel_major.shape[0]
    parts = pixel_major.reshape((local_views, zs, ys) + pixel_major.shape[2:])
    parts = lax.all_to_all(parts, "vy", split_axis=2, concat_axis=0, tiled=True)
    parts = lax.all_to_all(parts, "vz", split_axis=1, concat_axis=1, tiled=True)
    parts = jnp.swapaxes(parts, 0, 1)
    return parts.reshape((zs * ys * local_views, 1) + pixel_major.shape[2:])


def local(
    latent,
    gn_gain,
    gn_bias,
    cam_idx,
    noise_idx,
    cam_table,
    noise_table,
    conv_w,
    conv_bias,
    ln_gain,
    attn_in,
    attn_out,
    head_scale,
):
    samples, local_views, local_rows, local_cols, channels = latent.shape
    width_out = ln_gain.shape[0]
    out_part = conv_w.shape[-1]
    whole = lax.all_gather(latent, ROW, axis=2, tiled=True)
    whole, attn_in = lax.optimization_barrier((whole, attn_in))
    core = lax.axis_index("core")
    half_in = attn_in.shape[1] // 2
    half_out = attn_out.shape[1] // 2
    in_half = lax.dynamic_slice_in_dim(attn_in, core * half_in, half_in, axis=1)
    in_half = lax.all_gather(in_half, VIEW, axis=0, tiled=False)
    out_half = lax.dynamic_slice_in_dim(attn_out, core * half_out, half_out, axis=1)
    view_devices = lax.axis_size(VIEW)
    out_half = jnp.broadcast_to(out_half[None], (view_devices,) + out_half.shape)
    out_half = lax.all_to_all(out_half, VIEW, split_axis=0, concat_axis=0, tiled=True)
    out_half = out_half.reshape(-1, half_out)

    all_rows = whole.shape[2]
    x_float = whole.astype(jnp.float32)
    grouped = x_float.reshape(
        samples, local_views, all_rows, local_cols, GROUPS, channels // GROUPS
    )
    average = jnp.mean(grouped, axis=(2, 3, 5), keepdims=True)
    centred = grouped - average
    variance = jnp.mean(centred * centred, axis=(2, 3, 5), keepdims=True)
    normed = (centred * lax.rsqrt(variance + epsilon)).reshape(x_float.shape)
    cam_film = jnp.take(cam_table, cam_idx, axis=0).astype(jnp.float32)
    noise_film = jnp.take(noise_table, noise_idx, axis=0).astype(jnp.float32)
    film_rows = cam_film + noise_film[:, None, :]
    film_scale = film_rows[:, :, None, None, :channels]
    film_shift = film_rows[:, :, None, None, channels:]
    hidden = (normed * gn_gain + gn_bias) * (1.0 + film_scale) + film_shift
    activated = jax.nn.silu(hidden).astype(jnp.bfloat16)
    out_half, activated = lax.optimization_barrier((out_half, activated))
    taps = conv_w.shape[1]
    padded = jnp.pad(activated, ((0, 0), (0, 0), (1, 1), (0, 0), (0, 0)))
    tap_sum = None
    for tap_row in range(conv_w.shape[0]):
        rows_in = padded[:, :, tap_row : tap_row + all_rows].reshape(-1, channels)
        weight_row = jnp.transpose(conv_w[tap_row], (1, 0, 2)).reshape(channels, taps * out_part)
        part = jnp.dot(rows_in, weight_row, preferred_element_type=jnp.float32)
        tap_sum = part if tap_sum is None else tap_sum + part
    tap_sum = tap_sum.reshape(samples, local_views, all_rows, local_cols, taps, out_part)
    wide = jnp.pad(tap_sum, ((0, 0), (0, 0), (0, 0), (1, 1), (0, 0), (0, 0)))
    conv_out = (
        wide[:, :, :, 0:local_cols, 0]
        + wide[:, :, :, 1 : local_cols + 1, 1]
        + wide[:, :, :, 2 : local_cols + 2, 2]
    )
    me = lax.axis_index("chip") * lax.axis_size("core") + core
    conv_part = conv_out.astype(jnp.bfloat16)
    conv_rows = lax.all_to_all(conv_part, ROW, split_axis=2, concat_axis=4, tiled=True)
    resid_out = (
        latent.astype(jnp.float32) + conv_rows.astype(jnp.float32) + conv_bias
    ).astype(jnp.bfloat16)
    resid_float = resid_out.astype(jnp.float32)
    middle = jnp.mean(resid_float, axis=-1, keepdims=True)
    spread_y = jnp.mean((resid_float - middle) ** 2, axis=-1, keepdims=True)
    normed_y = ((resid_float - middle) * lax.rsqrt(spread_y + epsilon) * ln_gain).astype(
        jnp.bfloat16
    )
    view_devices = lax.axis_size(VIEW)
    per_device = samples * local_rows * local_cols // view_devices
    pixel_major = jnp.moveaxis(normed_y, 1, 0).reshape(
        local_views, view_devices, per_device, width_out
    )
    views = send_out(pixel_major)
    in_half, views = lax.optimization_barrier((in_half, views))
    swap = [(0, 1), (1, 0)]
    in_other = lax.ppermute(in_half, "core", swap)
    flat_block = views.reshape(-1, width_out)
    block_mine = lax.dynamic_slice_in_dim(flat_block, core * half_in, half_in, axis=1)
    block_other = lax.dynamic_slice_in_dim(flat_block, (1 - core) * half_in, half_in, axis=1)
    triple_in = jnp.einsum(
        "pc,jmcd->mpjd", block_mine, in_half, preferred_element_type=jnp.float32
    ) + jnp.einsum(
        "pc,jmcd->mpjd", block_other, in_other, preferred_element_type=jnp.float32
    )
    triple_in = triple_in.astype(jnp.bfloat16).reshape((3,) + views.shape)
    mixed = send_back(attend(triple_in[0], triple_in[1], triple_in[2], head_scale))
    out_half, mixed = lax.optimization_barrier((out_half, mixed))
    out_other = lax.ppermute(out_half, "core", swap)
    mixed = jnp.moveaxis(
        mixed.reshape(local_views, samples, local_rows, local_cols, width_out), 0, 1
    )
    flat_mixed = mixed.reshape(-1, width_out)
    cols_mine = jnp.dot(flat_mixed, out_half, preferred_element_type=jnp.float32)
    cols_other = jnp.dot(flat_mixed, out_other, preferred_element_type=jnp.float32)
    projected = jnp.where(
        core == 0,
        jnp.concatenate([cols_mine, cols_other], axis=1),
        jnp.concatenate([cols_other, cols_mine], axis=1),
    )
    return (resid_float + projected.reshape(resid_float.shape)).astype(jnp.bfloat16)

ROW = ("chip", "core")
VIEW = ("vz", "vy")


def solution(mesh):
    cores = 2
    split = jax.sharding.Mesh(
        mesh.devices.reshape(
            mesh.shape["view"] // 2, 2, mesh.shape["row"] // cores, cores
        ),
        ("vz", "vy", "chip", "core"),
    )
    placed = (
        P(None, VIEW, ROW, None, None),
        P(),
        P(),
        P(None, VIEW),
        P(),
        P(),
        P(),
        P(None, None, None, ROW),
        P(),
        P(),
        P(None, None, VIEW),
        P(VIEW, None),
        P(),
    )
    return jax.shard_map(
        local,
        mesh=split,
        in_specs=placed,
        out_specs=P(None, VIEW, ROW, None, None),
        check_vma=False,
    )
```

```python
import math

import jax
import jax.numpy as jnp
from jax import lax
from jax.sharding import PartitionSpec as P

GROUPS = 32


epsilon = 1e-05


def attend(query, key_block, value, head_scale):
    view_count = query.shape[0]
    item_count = query.shape[2]
    channels = query.shape[3]
    head_count = head_scale.shape[0]
    head_size = channels // head_count
    query_heads = query.reshape(view_count, item_count, head_count, head_size)
    key_heads = key_block.reshape(view_count, item_count, head_count, head_size)
    value_heads = value.reshape(view_count, item_count, head_count, head_size)
    scores = jnp.einsum(
        "vihd,uihd->ihvu", query_heads, key_heads, preferred_element_type=jnp.float32
    )
    scores = scores * (head_scale / math.sqrt(head_size))[None, :, None, None]
    peak_score = jnp.max(scores, axis=-1, keepdims=True)
    exp_scores = jnp.exp(scores - peak_score)
    soft_weights = (exp_scores / jnp.sum(exp_scores, axis=-1, keepdims=True)).astype(jnp.bfloat16)
    mixed = jnp.einsum(
        "ihvu,uihd->vihd", soft_weights, value_heads, preferred_element_type=jnp.float32
    )
    return mixed.astype(jnp.bfloat16).reshape(view_count, 1, item_count, channels)


def send_back(mixed):
    return lax.all_to_all(mixed, VIEW, split_axis=0, concat_axis=1, tiled=True)


def send_out(pixel_major):
    ys = lax.axis_size("vy")
    zs = lax.axis_size("vz")
    local_views = pixel_major.shape[0]
    parts = pixel_major.reshape((local_views, zs, ys) + pixel_major.shape[2:])
    parts = lax.all_to_all(parts, "vy", split_axis=2, concat_axis=0, tiled=True)
    parts = lax.all_to_all(parts, "vz", split_axis=1, concat_axis=1, tiled=True)
    parts = jnp.swapaxes(parts, 0, 1)
    return parts.reshape((zs * ys * local_views, 1) + pixel_major.shape[2:])


def local(
    latent,
    gn_gain,
    gn_bias,
    cam_idx,
    noise_idx,
    cam_table,
    noise_table,
    conv_w,
    conv_bias,
    ln_gain,
    attn_in,
    attn_out,
    head_scale,
):
    samples, local_views, local_rows, local_cols, channels = latent.shape
    width_out = ln_gain.shape[0]
    out_part = conv_w.shape[-1]
    whole = lax.all_gather(latent, ROW, axis=2, tiled=True)
    whole, attn_in = lax.optimization_barrier((whole, attn_in))
    core = lax.axis_index("core")
    half_in = attn_in.shape[1] // 2
    half_out = attn_out.shape[1] // 2
    in_half = lax.dynamic_slice_in_dim(attn_in, core * half_in, half_in, axis=1)
    in_half = lax.all_gather(in_half, VIEW, axis=0, tiled=False)
    out_half = lax.dynamic_slice_in_dim(attn_out, core * half_out, half_out, axis=1)
    view_devices = lax.axis_size(VIEW)
    out_half = jnp.broadcast_to(out_half[None], (view_devices,) + out_half.shape)
    out_half = lax.all_to_all(out_half, VIEW, split_axis=0, concat_axis=0, tiled=True)
    out_half = out_half.reshape(-1, half_out)

    all_rows = whole.shape[2]
    x_float = whole.astype(jnp.float32)
    grouped = x_float.reshape(
        samples, local_views, all_rows, local_cols, GROUPS, channels // GROUPS
    )
    average = jnp.mean(grouped, axis=(2, 3, 5), keepdims=True)
    centred = grouped - average
    variance = jnp.mean(centred * centred, axis=(2, 3, 5), keepdims=True)
    normed = (centred * lax.rsqrt(variance + epsilon)).reshape(x_float.shape)
    cam_film = jnp.take(cam_table, cam_idx, axis=0).astype(jnp.float32)
    noise_film = jnp.take(noise_table, noise_idx, axis=0).astype(jnp.float32)
    film_rows = cam_film + noise_film[:, None, :]
    film_scale = film_rows[:, :, None, None, :channels]
    film_shift = film_rows[:, :, None, None, channels:]
    hidden = (normed * gn_gain + gn_bias) * (1.0 + film_scale) + film_shift
    activated = jax.nn.silu(hidden).astype(jnp.bfloat16)
    out_half, activated = lax.optimization_barrier((out_half, activated))
    swap = [(0, 1), (1, 0)]
    out_other = lax.ppermute(out_half, "core", swap)
    taps = conv_w.shape[1]
    padded = jnp.pad(activated, ((0, 0), (0, 0), (1, 1), (0, 0), (0, 0)))
    tap_sum = None
    for tap_row in range(conv_w.shape[0]):
        rows_in = padded[:, :, tap_row : tap_row + all_rows].reshape(-1, channels)
        weight_row = jnp.transpose(conv_w[tap_row], (1, 0, 2)).reshape(channels, taps * out_part)
        part = jnp.dot(rows_in, weight_row, preferred_element_type=jnp.float32)
        tap_sum = part if tap_sum is None else tap_sum + part
    tap_sum = tap_sum.reshape(samples, local_views, all_rows, local_cols, taps, out_part)
    wide = jnp.pad(tap_sum, ((0, 0), (0, 0), (0, 0), (1, 1), (0, 0), (0, 0)))
    conv_out = (
        wide[:, :, :, 0:local_cols, 0]
        + wide[:, :, :, 1 : local_cols + 1, 1]
        + wide[:, :, :, 2 : local_cols + 2, 2]
    )
    me = lax.axis_index("chip") * lax.axis_size("core") + core
    conv_part = conv_out.astype(jnp.bfloat16)
    conv_rows = lax.all_to_all(conv_part, ROW, split_axis=2, concat_axis=4, tiled=True)
    out_other, conv_rows = lax.optimization_barrier((out_other, conv_rows))
    resid_out = (
        latent.astype(jnp.float32) + conv_rows.astype(jnp.float32) + conv_bias
    ).astype(jnp.bfloat16)
    resid_float = resid_out.astype(jnp.float32)
    middle = jnp.mean(resid_float, axis=-1, keepdims=True)
    spread_y = jnp.mean((resid_float - middle) ** 2, axis=-1, keepdims=True)
    normed_y = ((resid_float - middle) * lax.rsqrt(spread_y + epsilon) * ln_gain).astype(
        jnp.bfloat16
    )
    view_devices = lax.axis_size(VIEW)
    per_device = samples * local_rows * local_cols // view_devices
    pixel_major = jnp.moveaxis(normed_y, 1, 0).reshape(
        local_views, view_devices, per_device, width_out
    )
    views = send_out(pixel_major)
    in_half, views = lax.optimization_barrier((in_half, views))
    in_other = lax.ppermute(in_half, "core", swap)
    flat_block = views.reshape(-1, width_out)
    block_mine = lax.dynamic_slice_in_dim(flat_block, core * half_in, half_in, axis=1)
    block_other = lax.dynamic_slice_in_dim(flat_block, (1 - core) * half_in, half_in, axis=1)
    triple_in = jnp.einsum(
        "pc,jmcd->mpjd", block_mine, in_half, preferred_element_type=jnp.float32
    ) + jnp.einsum(
        "pc,jmcd->mpjd", block_other, in_other, preferred_element_type=jnp.float32
    )
    triple_in = triple_in.astype(jnp.bfloat16).reshape((3,) + views.shape)
    mixed = send_back(attend(triple_in[0], triple_in[1], triple_in[2], head_scale))
    mixed = jnp.moveaxis(
        mixed.reshape(local_views, samples, local_rows, local_cols, width_out), 0, 1
    )
    flat_mixed = mixed.reshape(-1, width_out)
    cols_mine = jnp.dot(flat_mixed, out_half, preferred_element_type=jnp.float32)
    cols_other = jnp.dot(flat_mixed, out_other, preferred_element_type=jnp.float32)
    projected = jnp.where(
        core == 0,
        jnp.concatenate([cols_mine, cols_other], axis=1),
        jnp.concatenate([cols_other, cols_mine], axis=1),
    )
    return (resid_float + projected.reshape(resid_float.shape)).astype(jnp.bfloat16)

ROW = ("chip", "core")
VIEW = ("vz", "vy")


def solution(mesh):
    cores = 2
    split = jax.sharding.Mesh(
        mesh.devices.reshape(
            mesh.shape["view"] // 2, 2, mesh.shape["row"] // cores, cores
        ),
        ("vz", "vy", "chip", "core"),
    )
    placed = (
        P(None, VIEW, ROW, None, None),
        P(),
        P(),
        P(None, VIEW),
        P(),
        P(),
        P(),
        P(None, None, None, ROW),
        P(),
        P(),
        P(None, None, VIEW),
        P(VIEW, None),
        P(),
    )
    return jax.shard_map(
        local,
        mesh=split,
        in_specs=placed,
        out_specs=P(None, VIEW, ROW, None, None),
        check_vma=False,
    )
```
